512 devices in a mesh: grp: 4 (over x), gx: 16 (over z_hi, y), gy: 8 (over z_lo, core).
Axes of the slice: x: 4, y: 8, z: 8 (z_hi: 2, z_lo: 4; z = z_hi * 4 + z_lo), core: 2. Of those that a mesh axis runs over, the one named last changes fastest.
Arguments:
- fwd_now: float32 [3, 64, 64, 128], P(None, 'gx', 'gy'), may hold values from -6 to 6
- fwd_prev: float32 [3, 64, 64, 128], P(None, 'gx', 'gy'), may hold values from -6 to 6
- adj_now: float32 [16, 3, 64, 64, 128], P('grp', None, 'gx', 'gy'), may hold values from -6 to 6
- adj_prev: float32 [16, 3, 64, 64, 128], P('grp', None, 'gx', 'gy'), may hold values from -6 to 6
- lame_first: float32 [64, 64, 128], P('gx', 'gy'), may hold values from 0.5 to 2
- shear_mod: float32 [64, 64, 128], P('gx', 'gy'), may hold values from 0.3 to 1.2
- buoyancy: float32 [64, 64, 128], P('gx', 'gy'), may hold values from 0.5 to 1
- master_cell: int32 [1], replicated, may hold values from 0 to 524287
- master_lag: int32 [1], replicated, may hold values from 0 to 254
- master_trace: float32 [256, 3], replicated, may hold values from -96 to 96
- receiver_cell: int32 [16], P('grp'), may hold values from 0 to 524287
- receiver_lag: int32 [16], P('grp'), may hold values from 0 to 254
- receiver_trace: float32 [16, 256, 3], P('grp'), may hold values from -96 to 96
Outputs:
- adj_final: float32 [16, 3, 64, 64, 128], P('grp', None, 'gx', 'gy')
- kernels: float32 [2, 64, 64, 128], P(None, 'gx', 'gy', 'grp')
The draws below stay inside these ranges and needn't reach their ends.
Inputs may be any that keep to these rules, and one draw needn't show every extreme that they name: `receiver_cell`: cell index in the whole grid, numbered (x * 64 + y) * 128 + z. `master_cell`: cell index in the whole grid, numbered (x * 64 + y) * 128 + z.
All inputs are finite; a program needn't handle non-finite values.
Results may differ from the reference program's by a relative error of at most 0.00011.
Values sent between devices are 32-bit elements; how exact they have to be, the bound alone decides.
No kernel may reach another device: no remote copies, remote signals or barrier semaphores. Data moves between devices by JAX's collectives and lax.ppermute only.
A program may use at most 64 MiB of HBM per device.

```python
import math
import jax
import jax.numpy as jnp
from jax import lax

NZ = 128
STEPS = 2
TRACE = 256
NX = 64
NY = 64
RCV_ALL = 16


def set_ends(entries, rng, low, largest):
    extent = entries.shape
    spot = [jax.random.randint(jax.random.fold_in(rng, axis), (), 0, extent[axis]) for axis in range(len(extent))]
    entries = entries.at[tuple(spot)].set(low)
    longest = extent.index(max(extent))
    spot[longest] = (spot[longest] + 1) % extent[longest]
    return entries.at[tuple(spot)].set(largest)


def levels(rng, extent, shards, smallest, high):
    level = 1.0
    for dim, parts in shards:
        draws = jax.random.uniform(jax.random.fold_in(jax.random.fold_in(rng, 6), dim), (parts,), jnp.float32, smallest / len(shards), high / len(shards))
        level = level * jnp.repeat(jnp.exp(draws), extent[dim] // parts).reshape((-1,) + (1,) * (len(extent) - 1 - dim))
    return level


def noise(key, shape, spread, limit, pieces=(), kind=jnp.bfloat16):
    entries = jax.random.normal(key, shape, jnp.float32) * spread
    if len(pieces) > 0:
        entries = levels(key, shape, pieces, -0.22, 0.18) * entries
    return jnp.clip(entries, min=-limit, max=limit).astype(kind)


def setup_inputs(seed: int = 0) -> dict:
    streams_of = jax.random.split(jax.random.key(seed), 14)
    fwd_now = noise(streams_of[0], (3, NX, NY, NZ), 1.0, 6.0, ((1, 16), (2, 8)), jnp.float32)
    fwd_prev = noise(streams_of[1], (3, NX, NY, NZ), 1.0, 6.0, ((1, 16), (2, 8)), jnp.float32)
    adj_now = noise(streams_of[2], (RCV_ALL, 3, NX, NY, NZ), 1.0, 6.0, ((0, 4), (2, 16), (3, 8)), jnp.float32)
    adj_prev = noise(streams_of[3], (RCV_ALL, 3, NX, NY, NZ), 1.0, 6.0, ((0, 4), (2, 16), (3, 8)), jnp.float32)
    lame_first = jnp.clip(jnp.exp(math.log(2.0) - 1.3862944 * jax.random.uniform(streams_of[4], (NX, NY, NZ), jnp.float32) ** levels(streams_of[4], (NX, NY, NZ), ((0, 16), (1, 8)), -0.2, 0.2)), 0.5, 2.0)
    shear_mod = jnp.clip(jnp.exp(math.log(1.2) - 1.3862944 * jax.random.uniform(streams_of[5], (NX, NY, NZ), jnp.float32) ** levels(streams_of[5], (NX, NY, NZ), ((0, 16), (1, 8)), -0.2, 0.2)), 0.3, 1.2)
    buoyancy = jnp.clip(jnp.exp(math.log(1.0) - 0.6931472 * jax.random.uniform(streams_of[6], (NX, NY, NZ), jnp.float32) ** levels(streams_of[6], (NX, NY, NZ), ((0, 16), (1, 8)), -0.2, 0.2)), 0.5, 1.0)
    master_cell = jax.random.randint(streams_of[7], (1,), 0, NX * NY * NZ).astype(jnp.int32)
    master_lag = jax.random.randint(streams_of[8], (1,), 0, TRACE - STEPS + 1).astype(jnp.int32)
    master_trace = noise(streams_of[9], (TRACE, 3), 16.0, 96.0, (), jnp.float32)
    receiver_cell = set_ends(jax.random.randint(streams_of[10], (RCV_ALL,), 0, NX * NY * NZ), jax.random.fold_in(streams_of[10], 1), 0, (NX * NY * NZ) - 1).astype(jnp.int32)
    receiver_lag = set_ends(jax.random.randint(streams_of[11], (RCV_ALL,), 0, TRACE - STEPS + 1), jax.random.fold_in(streams_of[11], 1), 0, TRACE - STEPS).astype(jnp.int32)
    receiver_trace = noise(streams_of[12], (RCV_ALL, TRACE, 3), 16.0, 96.0, ((0, 4),), jnp.float32)
    return {"fwd_now": fwd_now, "fwd_prev": fwd_prev, "adj_now": adj_now, "adj_prev": adj_prev, "lame_first": lame_first, "shear_mod": shear_mod, "buoyancy": buoyancy, "master_cell": master_cell, "master_lag": master_lag, "master_trace": master_trace, "receiver_cell": receiver_cell, "receiver_lag": receiver_lag, "receiver_trace": receiver_trace}


time_step_sq = 0.0625


def backward_diff(stress, axis):
    upper = stress[:, 1:, 1:, 1:]
    if axis == 1:
        lower = stress[:, :-1, 1:, 1:]
    elif axis == 2:
        lower = stress[:, 1:, :-1, 1:]
    else:
        lower = stress[:, 1:, 1:, :-1]
    return upper - lower


def stencil(padded, lame_pad, shear_pad):
    span_x = padded.shape[2] - 2
    span_y = padded.shape[3] - 2
    span_z = padded.shape[4] - 2
    anchor = padded[:, :, :span_x + 1, :span_y + 1, :span_z + 1]
    grad_x = padded[:, :, 1:, :span_y + 1, :span_z + 1] - anchor
    grad_y = padded[:, :, :span_x + 1, 1:, :span_z + 1] - anchor
    grad_z = padded[:, :, :span_x + 1, :span_y + 1, 1:] - anchor
    strain_xx = grad_x[:, 0]
    strain_yy = grad_y[:, 1]
    strain_zz = grad_z[:, 2]
    strain_xy = 0.5 * (grad_y[:, 0] + grad_x[:, 1])
    strain_xz = 0.5 * (grad_z[:, 0] + grad_x[:, 2])
    strain_yz = 0.5 * (grad_z[:, 1] + grad_y[:, 2])
    lame = lame_pad[:span_x + 1, :span_y + 1, :span_z + 1]
    shear = shear_pad[:span_x + 1, :span_y + 1, :span_z + 1]
    dilation = strain_xx + strain_yy + strain_zz
    stress_xx = lame * dilation + 2.0 * shear * strain_xx
    stress_yy = lame * dilation + 2.0 * shear * strain_yy
    stress_zz = lame * dilation + 2.0 * shear * strain_zz
    stress_xy = 2.0 * shear * strain_xy
    stress_xz = 2.0 * shear * strain_xz
    stress_yz = 2.0 * shear * strain_yz
    force_x = backward_diff(stress_xx, 1) + backward_diff(stress_xy, 2) + backward_diff(stress_xz, 3)
    force_y = backward_diff(stress_xy, 1) + backward_diff(stress_yy, 2) + backward_diff(stress_yz, 3)
    force_z = backward_diff(stress_xz, 1) + backward_diff(stress_yz, 2) + backward_diff(stress_zz, 3)
    force = jnp.stack([force_x, force_y, force_z], axis=1)
    strain = jnp.stack([strain_xx, strain_yy, strain_zz, strain_xy, strain_xz, strain_yz], axis=1)
    return force, strain[:, :, 1:, 1:, 1:]


def reference(fwd_now, fwd_prev, adj_now, adj_prev, lame_first, shear_mod, buoyancy, master_cell, master_lag, master_trace, receiver_cell, receiver_lag, receiver_trace):
    lame_pad = jnp.pad(lame_first, 1)
    shear_pad = jnp.pad(shear_mod, 1)
    weights = jnp.array([1.0, 1.0, 1.0, 2.0, 2.0, 2.0], jnp.float32)[:, None, None, None]

    def advance(current, earlier, cell, lag, trace, instant):
        padded = jnp.pad(current, ((0, 0), (1, 1), (1, 1), (1, 1)))[None]
        force, strain = stencil(padded, lame_pad, shear_pad)
        amplitude = lax.dynamic_index_in_dim(trace, lag + instant, 0, keepdims=False)
        placed = jnp.zeros((NX * NY * NZ,), jnp.float32).at[cell].add(1.0).reshape(NX, NY, NZ)
        source = amplitude[:, None, None, None] * placed[None]
        following = 2.0 * current - earlier + time_step_sq * buoyancy * (force[0] + source)
        return following, strain[0]

    master_strains = []
    current, earlier = fwd_now, fwd_prev
    for instant in range(STEPS):
        following, strain = advance(current, earlier, master_cell[0], master_lag[0], master_trace, instant)
        master_strains.append(strain)
        current, earlier = following, current

    def one_receiver(packed):
        current, earlier, cell, lag, trace = packed
        dilation_term = jnp.zeros((NX, NY, NZ), jnp.float32)
        shear_term = jnp.zeros((NX, NY, NZ), jnp.float32)
        for instant in range(STEPS):
            following, strain = advance(current, earlier, cell, lag, trace, instant)
            master = master_strains[instant]
            dilation_term = dilation_term + (master[0] + master[1] + master[2]) * (strain[0] + strain[1] + strain[2])
            shear_term = shear_term + 2.0 * jnp.sum(weights * master * strain, axis=0)
            current, earlier = following, current
        return current, dilation_term, shear_term

    finals, dilation_terms, shear_terms = lax.map(one_receiver, (adj_now, adj_prev, receiver_cell, receiver_lag, receiver_trace))
    scale_out = 1.0 / (STEPS * RCV_ALL)
    kernels = jnp.stack([jnp.sum(dilation_terms, axis=0), jnp.sum(shear_terms, axis=0)]) * scale_out
    return finals, kernels
```

```python
import jax
import jax.numpy as jnp
from jax import lax
from jax.sharding import PartitionSpec as P

STEPS = 2


time_step_sq = 0.0625


def with_halo(cells, sides, width):
    for axis, dim in sides:
        count = lax.axis_size(axis)
        ends = count - 1
        head = lax.slice_in_dim(cells, 0, width, axis=dim)
        tail = lax.slice_in_dim(cells, cells.shape[dim] - width, cells.shape[dim], axis=dim)
        cells = jnp.concatenate(
            [
                lax.ppermute(tail, axis, [(i, i + 1) for i in range(ends)]),
                cells,
                lax.ppermute(head, axis, [(i + 1, i) for i in range(ends)]),
            ],
            axis=dim,
        )
    return cells


def backward_diff(stress, axis):
    upper = stress[:, 1:, 1:, 1:]
    if axis == 1:
        lower = stress[:, :-1, 1:, 1:]
    elif axis == 2:
        lower = stress[:, 1:, :-1, 1:]
    else:
        lower = stress[:, 1:, 1:, :-1]
    return upper - lower


def strains_of(padded):
    span_x = padded.shape[2] - 2
    span_y = padded.shape[3] - 2
    span_z = padded.shape[4] - 2
    anchor = padded[:, :, : span_x + 1, : span_y + 1, : span_z + 1]
    grad_x = padded[:, :, 1:, : span_y + 1, : span_z + 1] - anchor
    grad_y = padded[:, :, : span_x + 1, 1:, : span_z + 1] - anchor
    grad_z = padded[:, :, : span_x + 1, : span_y + 1, 1:] - anchor
    strain_xx = grad_x[:, 0]
    strain_yy = grad_y[:, 1]
    strain_zz = grad_z[:, 2]
    strain_xy = 0.5 * (grad_y[:, 0] + grad_x[:, 1])
    strain_xz = 0.5 * (grad_z[:, 0] + grad_x[:, 2])
    strain_yz = 0.5 * (grad_z[:, 1] + grad_y[:, 2])
    return strain_xx, strain_yy, strain_zz, strain_xy, strain_xz, strain_yz


def stencil(padded, lame_pad, shear_pad):
    span_x = padded.shape[2] - 2
    span_y = padded.shape[3] - 2
    span_z = padded.shape[4] - 2
    strain_xx, strain_yy, strain_zz, strain_xy, strain_xz, strain_yz = strains_of(padded)
    lame = lame_pad[: span_x + 1, : span_y + 1, : span_z + 1]
    shear = shear_pad[: span_x + 1, : span_y + 1, : span_z + 1]
    dilation = strain_xx + strain_yy + strain_zz
    stress_xx = lame * dilation + 2.0 * shear * strain_xx
    stress_yy = lame * dilation + 2.0 * shear * strain_yy
    stress_zz = lame * dilation + 2.0 * shear * strain_zz
    stress_xy = 2.0 * shear * strain_xy
    stress_xz = 2.0 * shear * strain_xz
    stress_yz = 2.0 * shear * strain_yz
    force_x = (
        backward_diff(stress_xx, 1) + backward_diff(stress_xy, 2) + backward_diff(stress_xz, 3)
    )
    force_y = (
        backward_diff(stress_xy, 1) + backward_diff(stress_yy, 2) + backward_diff(stress_yz, 3)
    )
    force_z = (
        backward_diff(stress_xz, 1) + backward_diff(stress_yz, 2) + backward_diff(stress_zz, 3)
    )
    force = jnp.stack([force_x, force_y, force_z], axis=1)
    strain = jnp.stack([strain_xx, strain_yy, strain_zz, strain_xy, strain_xz, strain_yz], axis=1)
    return (force, strain[:, :, 1:, 1:, 1:])


def zpad(cells):
    widths = [(0, 0)] * (cells.ndim - 1) + [(1, 1)]
    return jnp.pad(cells, widths)


def locate(cells, start_x, start_y, width_y, depth, span_x, span_y):
    coord_x = cells // (width_y * depth) - start_x
    coord_y = cells // depth % width_y - start_y
    coord_z = cells % depth
    index_x = lax.broadcasted_iota(jnp.int32, (1, span_x, 1, 1), 1)
    index_y = lax.broadcasted_iota(jnp.int32, (1, 1, span_y, 1), 2)
    index_z = lax.broadcasted_iota(jnp.int32, (1, 1, 1, depth), 3)
    found = (
        (index_x == coord_x[:, None, None, None])
        & (index_y == coord_y[:, None, None, None])
        & (index_z == coord_z[:, None, None, None])
    )
    return found.astype(jnp.float32)


def pick(trace, lags):
    positions = lax.broadcasted_iota(jnp.int32, (1, trace.shape[1]), 1)
    chosen = positions == lags[:, None]
    return jnp.sum(jnp.where(chosen[:, :, None], trace, 0.0), axis=1)


def advance(current, earlier, force, amplitudes, masks, buoyancy):
    source = amplitudes[:, :, None, None, None] * masks[:, None]
    return 2.0 * current - earlier + time_step_sq * buoyancy * (force + source)


def local(
    fwd_now,
    fwd_prev,
    adj_now,
    adj_prev,
    lame_first,
    shear_mod,
    buoyancy,
    master_cell,
    master_lag,
    master_trace,
    receiver_cell,
    receiver_lag,
    receiver_trace,
):
    cells_x, cells_y, depth = lame_first.shape
    groups = lax.axis_size("grp")
    receivers = adj_now.shape[0]
    fields = receivers + 1
    width_y = cells_y * lax.axis_size("gy")
    start_x = lax.axis_index("gx") * cells_x
    start_y = lax.axis_index("gy") * cells_y
    grid = (cells_x, cells_y, depth)

    now = jnp.concatenate([fwd_now[None], adj_now]).reshape((fields * 3,) + grid)
    prev = jnp.concatenate([fwd_prev[None], adj_prev]).reshape((fields * 3,) + grid)
    moduli = jnp.stack([lame_first, shear_mod, buoyancy])
    stacked = jnp.concatenate([now, prev, moduli])
    grown = with_halo(stacked, (("gx", 1), ("gy", 2)), 2)
    now_grown = grown[: fields * 3].reshape((fields, 3) + grown.shape[1:])
    prev_grown = grown[fields * 3 : fields * 6].reshape((fields, 3) + grown.shape[1:])
    lame_grown = zpad(grown[fields * 6])
    shear_grown = zpad(grown[fields * 6 + 1])
    buoy_grown = grown[fields * 6 + 2]

    cells = jnp.concatenate([master_cell, receiver_cell])
    amps = [
        jnp.concatenate(
            [
                pick(master_trace[None], master_lag + instant),
                pick(receiver_trace, receiver_lag + instant),
            ]
        )
        for instant in range(STEPS)
    ]
    masks_wide = locate(
        cells, start_x - 1, start_y - 1, width_y, depth, cells_x + 2, cells_y + 2
    )
    masks = masks_wide[:, 1:-1, 1:-1]

    force0, strain0 = stencil(zpad(now_grown), lame_grown, shear_grown)
    now_wide = now_grown[:, :, 1:-1, 1:-1]
    next_wide = advance(
        now_wide,
        prev_grown[:, :, 1:-1, 1:-1],
        force0,
        amps[0],
        masks_wide,
        buoy_grown[1:-1, 1:-1],
    )
    strain0 = strain0[:, :, 1:-1, 1:-1]

    force1, strain1 = stencil(
        zpad(next_wide[1:]), lame_grown[1:-1, 1:-1], shear_grown[1:-1, 1:-1]
    )
    master1 = stencil(zpad(next_wide[:1]), lame_grown[1:-1, 1:-1], shear_grown[1:-1, 1:-1])[1]
    final = advance(
        next_wide[1:, :, 1:-1, 1:-1],
        now_wide[1:, :, 1:-1, 1:-1],
        force1,
        amps[1][1:],
        masks[1:],
        buoy_grown[2:-2, 2:-2],
    )

    weights = jnp.array([1.0, 1.0, 1.0, 2.0, 2.0, 2.0], jnp.float32)[:, None, None, None]
    totals = jnp.zeros((2,) + grid, jnp.float32)
    for master, strain in ((strain0[0], strain0[1:]), (master1[0], strain1)):
        summed = jnp.sum(strain, axis=0)
        dilation_term = (master[0] + master[1] + master[2]) * (summed[0] + summed[1] + summed[2])
        shear_term = 2.0 * jnp.sum(weights * master * summed, axis=0)
        totals = totals + jnp.stack([dilation_term, shear_term])
    totals = totals * (1.0 / (STEPS * receivers * groups))

    share = depth // groups
    me = lax.axis_index("grp")
    kernels = lax.dynamic_slice_in_dim(totals, me * share, share, 3)
    for shift in range(1, groups):
        part = lax.dynamic_slice_in_dim(totals, (me + shift) % groups * share, share, 3)
        kernels = kernels + lax.ppermute(
            part, "grp", [(i, (i + shift) % groups) for i in range(groups)]
        )
    return (final, kernels)


def solution(mesh):
    in_specs = (
        P(None, "gx", "gy", None),
        P(None, "gx", "gy", None),
        P("grp", None, "gx", "gy", None),
        P("grp", None, "gx", "gy", None),
        P("gx", "gy", None),
        P("gx", "gy", None),
        P("gx", "gy", None),
        P(),
        P(),
        P(),
        P("grp"),
        P("grp"),
        P("grp", None, None),
    )
    out_specs = (P("grp", None, "gx", "gy", None), P(None, "gx", "gy", "grp"))
    return jax.shard_map(local, mesh=mesh, in_specs=in_specs, out_specs=out_specs, check_vma=False)
```

```python
import jax
import jax.numpy as jnp
from jax import lax
from jax.sharding import PartitionSpec as P

STEPS = 2


time_step_sq = 0.0625


def with_halo(cells, sides, width):
    for axis, dim in sides:
        count = lax.axis_size(axis)
        ends = count - 1
        head = lax.slice_in_dim(cells, 0, width, axis=dim)
        tail = lax.slice_in_dim(cells, cells.shape[dim] - width, cells.shape[dim], axis=dim)
        cells = jnp.concatenate(
            [
                lax.ppermute(tail, axis, [(i, i + 1) for i in range(ends)]),
                cells,
                lax.ppermute(head, axis, [(i + 1, i) for i in range(ends)]),
            ],
            axis=dim,
        )
    return cells


def backward_diff(stress, axis):
    upper = stress[:, 1:, 1:, 1:]
    if axis == 1:
        lower = stress[:, :-1, 1:, 1:]
    elif axis == 2:
        lower = stress[:, 1:, :-1, 1:]
    else:
        lower = stress[:, 1:, 1:, :-1]
    return upper - lower


def strains_of(padded):
    span_x = padded.shape[2] - 2
    span_y = padded.shape[3] - 2
    span_z = padded.shape[4] - 2
    anchor = padded[:, :, : span_x + 1, : span_y + 1, : span_z + 1]
    grad_x = padded[:, :, 1:, : span_y + 1, : span_z + 1] - anchor
    grad_y = padded[:, :, : span_x + 1, 1:, : span_z + 1] - anchor
    grad_z = padded[:, :, : span_x + 1, : span_y + 1, 1:] - anchor
    strain_xx = grad_x[:, 0]
    strain_yy = grad_y[:, 1]
    strain_zz = grad_z[:, 2]
    strain_xy = 0.5 * (grad_y[:, 0] + grad_x[:, 1])
    strain_xz = 0.5 * (grad_z[:, 0] + grad_x[:, 2])
    strain_yz = 0.5 * (grad_z[:, 1] + grad_y[:, 2])
    return strain_xx, strain_yy, strain_zz, strain_xy, strain_xz, strain_yz


def stencil(padded, lame_pad, shear_pad):
    span_x = padded.shape[2] - 2
    span_y = padded.shape[3] - 2
    span_z = padded.shape[4] - 2
    strain_xx, strain_yy, strain_zz, strain_xy, strain_xz, strain_yz = strains_of(padded)
    lame = lame_pad[: span_x + 1, : span_y + 1, : span_z + 1]
    shear = shear_pad[: span_x + 1, : span_y + 1, : span_z + 1]
    dilation = strain_xx + strain_yy + strain_zz
    stress_xx = lame * dilation + 2.0 * shear * strain_xx
    stress_yy = lame * dilation + 2.0 * shear * strain_yy
    stress_zz = lame * dilation + 2.0 * shear * strain_zz
    stress_xy = 2.0 * shear * strain_xy
    stress_xz = 2.0 * shear * strain_xz
    stress_yz = 2.0 * shear * strain_yz
    force_x = (
        backward_diff(stress_xx, 1) + backward_diff(stress_xy, 2) + backward_diff(stress_xz, 3)
    )
    force_y = (
        backward_diff(stress_xy, 1) + backward_diff(stress_yy, 2) + backward_diff(stress_yz, 3)
    )
    force_z = (
        backward_diff(stress_xz, 1) + backward_diff(stress_yz, 2) + backward_diff(stress_zz, 3)
    )
    force = jnp.stack([force_x, force_y, force_z], axis=1)
    strain = jnp.stack([strain_xx, strain_yy, strain_zz, strain_xy, strain_xz, strain_yz], axis=1)
    return (force, strain[:, :, 1:, 1:, 1:])


def zpad(cells):
    widths = [(0, 0)] * (cells.ndim - 1) + [(1, 1)]
    return jnp.pad(cells, widths)


def locate(cells, start_x, start_y, width_y, depth, span_x, span_y):
    coord_x = cells // (width_y * depth) - start_x
    coord_y = cells // depth % width_y - start_y
    coord_z = cells % depth
    index_x = lax.broadcasted_iota(jnp.int32, (1, span_x, 1, 1), 1)
    index_y = lax.broadcasted_iota(jnp.int32, (1, 1, span_y, 1), 2)
    index_z = lax.broadcasted_iota(jnp.int32, (1, 1, 1, depth), 3)
    found = (
        (index_x == coord_x[:, None, None, None])
        & (index_y == coord_y[:, None, None, None])
        & (index_z == coord_z[:, None, None, None])
    )
    return found.astype(jnp.float32)


def pick(trace, lags):
    positions = lax.broadcasted_iota(jnp.int32, (1, trace.shape[1]), 1)
    chosen = positions == lags[:, None]
    return jnp.sum(jnp.where(chosen[:, :, None], trace, 0.0), axis=1)


def advance(current, earlier, force, amplitudes, masks, buoyancy):
    source = amplitudes[:, :, None, None, None] * masks[:, None]
    return 2.0 * current - earlier + time_step_sq * buoyancy * (force + source)


def shifted(value, by_x, by_y):
    count_x = lax.axis_size("gx")
    count_y = lax.axis_size("gy")
    pairs = [
        (i * count_y + j, (i + by_x) * count_y + j + by_y)
        for i in range(count_x)
        for j in range(count_y)
        if 0 <= i + by_x < count_x and 0 <= j + by_y < count_y
    ]
    return lax.ppermute(value, ("gx", "gy"), pairs)


def exchange(stacked, pairs_lo, pairs_hi):
    channels, cells_x, cells_y, depth = stacked.shape
    plane = (cells_y, depth)
    wide_lo = stacked[:pairs_lo, cells_x - 2 :].reshape((-1,) + plane)
    thin_lo = stacked[pairs_lo:, cells_x - 1 :].reshape((-1,) + plane)
    wide_hi = stacked[:pairs_hi, :2].reshape((-1,) + plane)
    thin_hi = stacked[pairs_hi:, :1].reshape((-1,) + plane)
    from_lo = shifted(jnp.concatenate([wide_lo, thin_lo]), 1, 0)
    from_hi = shifted(jnp.concatenate([wide_hi, thin_hi]), -1, 0)
    from_y_lo = shifted(stacked[:, :, cells_y - 2 :], 0, 1)
    from_y_hi = shifted(stacked[:, :, :2], 0, -1)
    corner_ll = shifted(stacked[:, cells_x - 2 :, cells_y - 2 :], 1, 1)
    corner_lh = shifted(stacked[:, cells_x - 2 :, :2], 1, -1)
    corner_hl = shifted(stacked[:, :2, cells_y - 2 :], -1, 1)
    corner_hh = shifted(stacked[:, :2, :2], -1, -1)

    blank = jnp.zeros((channels - pairs_lo, 1) + plane, jnp.float32)
    rows_lo = jnp.concatenate(
        [
            from_lo[: pairs_lo * 2].reshape((pairs_lo, 2) + plane),
            jnp.concatenate([blank, from_lo[pairs_lo * 2 :].reshape((-1, 1) + plane)], axis=1),
        ]
    )
    blank = jnp.zeros((channels - pairs_hi, 1) + plane, jnp.float32)
    rows_hi = jnp.concatenate(
        [
            from_hi[: pairs_hi * 2].reshape((pairs_hi, 2) + plane),
            jnp.concatenate([from_hi[pairs_hi * 2 :].reshape((-1, 1) + plane), blank], axis=1),
        ]
    )
    band_lo = jnp.concatenate([corner_ll, rows_lo, corner_lh], axis=2)
    band_mid = jnp.concatenate([from_y_lo, stacked, from_y_hi], axis=2)
    band_hi = jnp.concatenate([corner_hl, rows_hi, corner_hh], axis=2)
    return jnp.concatenate([band_lo, band_mid, band_hi], axis=1)


def local(
    fwd_now,
    fwd_prev,
    adj_now,
    adj_prev,
    lame_first,
    shear_mod,
    buoyancy,
    master_cell,
    master_lag,
    master_trace,
    receiver_cell,
    receiver_lag,
    receiver_trace,
):
    cells_x, cells_y, depth = lame_first.shape
    groups = lax.axis_size("grp")
    receivers = adj_now.shape[0]
    fields = receivers + 1
    width_y = cells_y * lax.axis_size("gy")
    start_x = lax.axis_index("gx") * cells_x
    start_y = lax.axis_index("gy") * cells_y
    grid = (cells_x, cells_y, depth)
    comps = fields * 3

    now = jnp.concatenate([fwd_now[None], adj_now]).reshape((comps,) + grid)
    prev = jnp.concatenate([fwd_prev[None], adj_prev]).reshape((comps,) + grid)
    stacked = jnp.concatenate([now, lame_first[None], shear_mod[None], prev, buoyancy[None]])
    grown = exchange(stacked, comps + 2, comps)
    now_grown = grown[:comps].reshape((fields, 3) + grown.shape[1:])
    lame_grown = zpad(grown[comps])
    shear_grown = zpad(grown[comps + 1])
    prev_grown = grown[comps + 2 : 2 * comps + 2].reshape((fields, 3) + grown.shape[1:])
    buoy_grown = grown[2 * comps + 2]

    cells = jnp.concatenate([master_cell, receiver_cell])
    amps = [
        jnp.concatenate(
            [
                pick(master_trace[None], master_lag + instant),
                pick(receiver_trace, receiver_lag + instant),
            ]
        )
        for instant in range(STEPS)
    ]
    masks_wide = locate(
        cells, start_x - 1, start_y - 1, width_y, depth, cells_x + 2, cells_y + 2
    )
    masks = masks_wide[:, 1:-1, 1:-1]

    force0, strain0 = stencil(zpad(now_grown), lame_grown, shear_grown)
    now_wide = now_grown[:, :, 1:-1, 1:-1]
    next_wide = advance(
        now_wide,
        prev_grown[:, :, 1:-1, 1:-1],
        force0,
        amps[0],
        masks_wide,
        buoy_grown[1:-1, 1:-1],
    )
    strain0 = strain0[:, :, 1:-1, 1:-1]

    force1, strain1 = stencil(
        zpad(next_wide[1:]), lame_grown[1:-1, 1:-1], shear_grown[1:-1, 1:-1]
    )
    master1 = stencil(zpad(next_wide[:1]), lame_grown[1:-1, 1:-1], shear_grown[1:-1, 1:-1])[1]
    final = advance(
        next_wide[1:, :, 1:-1, 1:-1],
        now_wide[1:, :, 1:-1, 1:-1],
        force1,
        amps[1][1:],
        masks[1:],
        buoy_grown[2:-2, 2:-2],
    )

    weights = jnp.array([1.0, 1.0, 1.0, 2.0, 2.0, 2.0], jnp.float32)[:, None, None, None]
    totals = jnp.zeros((2,) + grid, jnp.float32)
    for master, strain in ((strain0[0], strain0[1:]), (master1[0], strain1)):
        summed = jnp.sum(strain, axis=0)
        dilation_term = (master[0] + master[1] + master[2]) * (summed[0] + summed[1] + summed[2])
        shear_term = 2.0 * jnp.sum(weights * master * summed, axis=0)
        totals = totals + jnp.stack([dilation_term, shear_term])
    totals = totals * (1.0 / (STEPS * receivers * groups))

    share = depth // groups
    parts = jnp.moveaxis(totals.reshape((2, cells_x, cells_y, groups, share)), 3, 0)
    kernels = jnp.sum(lax.all_to_all(parts, "grp", 0, 0, tiled=False), axis=0)
    return (final, kernels)


def solution(mesh):
    in_specs = (
        P(None, "gx", "gy", None),
        P(None, "gx", "gy", None),
        P("grp", None, "gx", "gy", None),
        P("grp", None, "gx", "gy", None),
        P("gx", "gy", None),
        P("gx", "gy", None),
        P("gx", "gy", None),
        P(),
        P(),
        P(),
        P("grp"),
        P("grp"),
        P("grp", None, None),
    )
    out_specs = (P("grp", None, "gx", "gy", None), P(None, "gx", "gy", "grp"))
    return jax.shard_map(local, mesh=mesh, in_specs=in_specs, out_specs=out_specs, check_vma=False)
```

```python
import jax
import jax.numpy as jnp
from jax import lax
from jax.sharding import PartitionSpec as P

STEPS = 2


time_step_sq = 0.0625


def with_halo(cells, sides, width):
    for axis, dim in sides:
        count = lax.axis_size(axis)
        ends = count - 1
        head = lax.slice_in_dim(cells, 0, width, axis=dim)
        tail = lax.slice_in_dim(cells, cells.shape[dim] - width, cells.shape[dim], axis=dim)
        cells = jnp.concatenate(
            [
                lax.ppermute(tail, axis, [(i, i + 1) for i in range(ends)]),
                cells,
                lax.ppermute(head, axis, [(i + 1, i) for i in range(ends)]),
            ],
            axis=dim,
        )
    return cells


def backward_diff(stress, axis):
    upper = stress[:, 1:, 1:, 1:]
    if axis == 1:
        lower = stress[:, :-1, 1:, 1:]
    elif axis == 2:
        lower = stress[:, 1:, :-1, 1:]
    else:
        lower = stress[:, 1:, 1:, :-1]
    return upper - lower


def strains_of(padded):
    span_x = padded.shape[2] - 2
    span_y = padded.shape[3] - 2
    span_z = padded.shape[4] - 2
    anchor = padded[:, :, : span_x + 1, : span_y + 1, : span_z + 1]
    grad_x = padded[:, :, 1:, : span_y + 1, : span_z + 1] - anchor
    grad_y = padded[:, :, : span_x + 1, 1:, : span_z + 1] - anchor
    grad_z = padded[:, :, : span_x + 1, : span_y + 1, 1:] - anchor
    strain_xx = grad_x[:, 0]
    strain_yy = grad_y[:, 1]
    strain_zz = grad_z[:, 2]
    strain_xy = 0.5 * (grad_y[:, 0] + grad_x[:, 1])
    strain_xz = 0.5 * (grad_z[:, 0] + grad_x[:, 2])
    strain_yz = 0.5 * (grad_z[:, 1] + grad_y[:, 2])
    return strain_xx, strain_yy, strain_zz, strain_xy, strain_xz, strain_yz


def stencil(padded, lame_pad, shear_pad):
    span_x = padded.shape[2] - 2
    span_y = padded.shape[3] - 2
    span_z = padded.shape[4] - 2
    strain_xx, strain_yy, strain_zz, strain_xy, strain_xz, strain_yz = strains_of(padded)
    lame = lame_pad[: span_x + 1, : span_y + 1, : span_z + 1]
    shear = shear_pad[: span_x + 1, : span_y + 1, : span_z + 1]
    dilation = strain_xx + strain_yy + strain_zz
    stress_xx = lame * dilation + 2.0 * shear * strain_xx
    stress_yy = lame * dilation + 2.0 * shear * strain_yy
    stress_zz = lame * dilation + 2.0 * shear * strain_zz
    stress_xy = 2.0 * shear * strain_xy
    stress_xz = 2.0 * shear * strain_xz
    stress_yz = 2.0 * shear * strain_yz
    force_x = (
        backward_diff(stress_xx, 1) + backward_diff(stress_xy, 2) + backward_diff(stress_xz, 3)
    )
    force_y = (
        backward_diff(stress_xy, 1) + backward_diff(stress_yy, 2) + backward_diff(stress_yz, 3)
    )
    force_z = (
        backward_diff(stress_xz, 1) + backward_diff(stress_yz, 2) + backward_diff(stress_zz, 3)
    )
    force = jnp.stack([force_x, force_y, force_z], axis=1)
    strain = jnp.stack([strain_xx, strain_yy, strain_zz, strain_xy, strain_xz, strain_yz], axis=1)
    return (force, strain[:, :, 1:, 1:, 1:])


def zpad(cells):
    widths = [(0, 0)] * (cells.ndim - 1) + [(1, 1)]
    return jnp.pad(cells, widths)


def locate(cells, start_x, start_y, width_y, depth, span_x, span_y):
    coord_x = cells // (width_y * depth) - start_x
    coord_y = cells // depth % width_y - start_y
    coord_z = cells % depth
    index_x = lax.broadcasted_iota(jnp.int32, (1, span_x, 1, 1), 1)
    index_y = lax.broadcasted_iota(jnp.int32, (1, 1, span_y, 1), 2)
    index_z = lax.broadcasted_iota(jnp.int32, (1, 1, 1, depth), 3)
    found = (
        (index_x == coord_x[:, None, None, None])
        & (index_y == coord_y[:, None, None, None])
        & (index_z == coord_z[:, None, None, None])
    )
    return found.astype(jnp.float32)


def pick(trace, lags):
    positions = lax.broadcasted_iota(jnp.int32, (1, trace.shape[1]), 1)
    chosen = positions == lags[:, None]
    return jnp.sum(jnp.where(chosen[:, :, None], trace, 0.0), axis=1)


def advance(current, earlier, force, amplitudes, masks, buoyancy):
    source = amplitudes[:, :, None, None, None] * masks[:, None]
    return 2.0 * current - earlier + time_step_sq * buoyancy * (force + source)


def local(
    fwd_now,
    fwd_prev,
    adj_now,
    adj_prev,
    lame_first,
    shear_mod,
    buoyancy,
    master_cell,
    master_lag,
    master_trace,
    receiver_cell,
    receiver_lag,
    receiver_trace,
):
    cells_x, cells_y, depth = lame_first.shape
    groups = lax.axis_size("grp")
    receivers = adj_now.shape[0]
    fields = receivers + 1
    width_y = cells_y * lax.axis_size("gy")
    start_x = lax.axis_index("gx") * cells_x
    start_y = lax.axis_index("gy") * cells_y
    grid = (cells_x, cells_y, depth)

    now = jnp.concatenate([fwd_now[None], adj_now]).reshape((fields * 3,) + grid)
    prev = jnp.concatenate([fwd_prev[None], adj_prev]).reshape((fields * 3,) + grid)
    moduli = jnp.stack([lame_first, shear_mod, buoyancy])
    stacked = jnp.concatenate([now, prev, moduli])
    grown = with_halo(stacked, (("gx", 1), ("gy", 2)), 2)
    now_grown = grown[: fields * 3].reshape((fields, 3) + grown.shape[1:])
    prev_grown = grown[fields * 3 : fields * 6].reshape((fields, 3) + grown.shape[1:])
    lame_grown = zpad(grown[fields * 6])
    shear_grown = zpad(grown[fields * 6 + 1])
    buoy_grown = grown[fields * 6 + 2]

    cells = jnp.concatenate([master_cell, receiver_cell])
    amps = [
        jnp.concatenate(
            [
                pick(master_trace[None], master_lag + instant),
                pick(receiver_trace, receiver_lag + instant),
            ]
        )
        for instant in range(STEPS)
    ]
    masks_wide = locate(
        cells, start_x - 1, start_y - 1, width_y, depth, cells_x + 2, cells_y + 2
    )
    masks = masks_wide[:, 1:-1, 1:-1]

    force0, strain0 = stencil(zpad(now_grown), lame_grown, shear_grown)
    now_wide = now_grown[:, :, 1:-1, 1:-1]
    next_wide = advance(
        now_wide,
        prev_grown[:, :, 1:-1, 1:-1],
        force0,
        amps[0],
        masks_wide,
        buoy_grown[1:-1, 1:-1],
    )
    strain0 = strain0[:, :, 1:-1, 1:-1]

    force1, strain1 = stencil(
        zpad(next_wide[1:]), lame_grown[1:-1, 1:-1], shear_grown[1:-1, 1:-1]
    )
    master1 = stencil(zpad(next_wide[:1]), lame_grown[1:-1, 1:-1], shear_grown[1:-1, 1:-1])[1]
    final = advance(
        next_wide[1:, :, 1:-1, 1:-1],
        now_wide[1:, :, 1:-1, 1:-1],
        force1,
        amps[1][1:],
        masks[1:],
        buoy_grown[2:-2, 2:-2],
    )

    weights = jnp.array([1.0, 1.0, 1.0, 2.0, 2.0, 2.0], jnp.float32)[:, None, None, None]
    totals = jnp.zeros((2,) + grid, jnp.float32)
    for master, strain in ((strain0[0], strain0[1:]), (master1[0], strain1)):
        summed = jnp.sum(strain, axis=0)
        dilation_term = (master[0] + master[1] + master[2]) * (summed[0] + summed[1] + summed[2])
        shear_term = 2.0 * jnp.sum(weights * master * summed, axis=0)
        totals = totals + jnp.stack([dilation_term, shear_term])
    totals = totals * (1.0 / (STEPS * receivers * groups))

    share = depth // groups
    parts = jnp.moveaxis(totals.reshape((2, cells_x, cells_y, groups, share)), 3, 0)
    kernels = jnp.sum(lax.all_to_all(parts, "grp", 0, 0, tiled=False), axis=0)
    return (final, kernels)


def solution(mesh):
    in_specs = (
        P(None, "gx", "gy", None),
        P(None, "gx", "gy", None),
        P("grp", None, "gx", "gy", None),
        P("grp", None, "gx", "gy", None),
        P("gx", "gy", None),
        P("gx", "gy", None),
        P("gx", "gy", None),
        P(),
        P(),
        P(),
        P("grp"),
        P("grp"),
        P("grp", None, None),
    )
    out_specs = (P("grp", None, "gx", "gy", None), P(None, "gx", "gy", "grp"))
    return jax.shard_map(local, mesh=mesh, in_specs=in_specs, out_specs=out_specs, check_vma=False)
```

```python
import jax
import jax.numpy as jnp
from jax import lax
from jax.sharding import PartitionSpec as P

STEPS = 2


time_step_sq = 0.0625


def with_halo(cells, sides, width):
    for axis, dim in sides:
        count = lax.axis_size(axis)
        ends = count - 1
        head = lax.slice_in_dim(cells, 0, width, axis=dim)
        tail = lax.slice_in_dim(cells, cells.shape[dim] - width, cells.shape[dim], axis=dim)
        cells = jnp.concatenate(
            [
                lax.ppermute(tail, axis, [(i, i + 1) for i in range(ends)]),
                cells,
                lax.ppermute(head, axis, [(i + 1, i) for i in range(ends)]),
            ],
            axis=dim,
        )
    return cells


def backward_diff(stress, axis):
    upper = stress[:, 1:, 1:, 1:]
    if axis == 1:
        lower = stress[:, :-1, 1:, 1:]
    elif axis == 2:
        lower = stress[:, 1:, :-1, 1:]
    else:
        lower = stress[:, 1:, 1:, :-1]
    return upper - lower


def strains_of(padded):
    span_x = padded.shape[2] - 2
    span_y = padded.shape[3] - 2
    span_z = padded.shape[4] - 2
    anchor = padded[:, :, : span_x + 1, : span_y + 1, : span_z + 1]
    grad_x = padded[:, :, 1:, : span_y + 1, : span_z + 1] - anchor
    grad_y = padded[:, :, : span_x + 1, 1:, : span_z + 1] - anchor
    grad_z = padded[:, :, : span_x + 1, : span_y + 1, 1:] - anchor
    strain_xx = grad_x[:, 0]
    strain_yy = grad_y[:, 1]
    strain_zz = grad_z[:, 2]
    strain_xy = 0.5 * (grad_y[:, 0] + grad_x[:, 1])
    strain_xz = 0.5 * (grad_z[:, 0] + grad_x[:, 2])
    strain_yz = 0.5 * (grad_z[:, 1] + grad_y[:, 2])
    return strain_xx, strain_yy, strain_zz, strain_xy, strain_xz, strain_yz


def stencil(padded, lame_pad, shear_pad):
    span_x = padded.shape[2] - 2
    span_y = padded.shape[3] - 2
    span_z = padded.shape[4] - 2
    strain_xx, strain_yy, strain_zz, strain_xy, strain_xz, strain_yz = strains_of(padded)
    lame = lame_pad[: span_x + 1, : span_y + 1, : span_z + 1]
    shear = shear_pad[: span_x + 1, : span_y + 1, : span_z + 1]
    dilation = strain_xx + strain_yy + strain_zz
    stress_xx = lame * dilation + 2.0 * shear * strain_xx
    stress_yy = lame * dilation + 2.0 * shear * strain_yy
    stress_zz = lame * dilation + 2.0 * shear * strain_zz
    stress_xy = 2.0 * shear * strain_xy
    stress_xz = 2.0 * shear * strain_xz
    stress_yz = 2.0 * shear * strain_yz
    force_x = (
        backward_diff(stress_xx, 1) + backward_diff(stress_xy, 2) + backward_diff(stress_xz, 3)
    )
    force_y = (
        backward_diff(stress_xy, 1) + backward_diff(stress_yy, 2) + backward_diff(stress_yz, 3)
    )
    force_z = (
        backward_diff(stress_xz, 1) + backward_diff(stress_yz, 2) + backward_diff(stress_zz, 3)
    )
    force = jnp.stack([force_x, force_y, force_z], axis=1)
    strain = jnp.stack([strain_xx, strain_yy, strain_zz, strain_xy, strain_xz, strain_yz], axis=1)
    return (force, strain[:, :, 1:, 1:, 1:])


def zpad(cells):
    widths = [(0, 0)] * (cells.ndim - 1) + [(1, 1)]
    return jnp.pad(cells, widths)


def locate(cells, start_x, start_y, width_y, depth, span_x, span_y):
    coord_x = cells // (width_y * depth) - start_x
    coord_y = cells // depth % width_y - start_y
    coord_z = cells % depth
    index_x = lax.broadcasted_iota(jnp.int32, (1, span_x, 1, 1), 1)
    index_y = lax.broadcasted_iota(jnp.int32, (1, 1, span_y, 1), 2)
    index_z = lax.broadcasted_iota(jnp.int32, (1, 1, 1, depth), 3)
    found = (
        (index_x == coord_x[:, None, None, None])
        & (index_y == coord_y[:, None, None, None])
        & (index_z == coord_z[:, None, None, None])
    )
    return found.astype(jnp.float32)


def pick(trace, lags):
    positions = lax.broadcasted_iota(jnp.int32, (1, trace.shape[1]), 1)
    chosen = positions == lags[:, None]
    return jnp.sum(jnp.where(chosen[:, :, None], trace, 0.0), axis=1)


def advance(current, earlier, force, amplitudes, masks, buoyancy):
    source = amplitudes[:, :, None, None, None] * masks[:, None]
    return 2.0 * current - earlier + time_step_sq * buoyancy * (force + source)


def local(
    fwd_now,
    fwd_prev,
    adj_now,
    adj_prev,
    lame_first,
    shear_mod,
    buoyancy,
    master_cell,
    master_lag,
    master_trace,
    receiver_cell,
    receiver_lag,
    receiver_trace,
):
    cells_x, cells_y, depth = lame_first.shape
    groups = lax.axis_size("grp")
    receivers = adj_now.shape[0]
    fields = receivers + 1
    width_y = cells_y * lax.axis_size("gy")
    start_x = lax.axis_index("gx") * cells_x
    start_y = lax.axis_index("gy") * cells_y
    grid = (cells_x, cells_y, depth)

    now = jnp.concatenate([fwd_now[None], adj_now]).reshape((fields * 3,) + grid)
    prev = jnp.concatenate([fwd_prev[None], adj_prev]).reshape((fields * 3,) + grid)
    moduli = jnp.stack([lame_first, shear_mod, buoyancy])
    stacked = jnp.concatenate([now, prev, moduli])
    grown = with_halo(stacked, (("gx", 1), ("gy", 2)), 2)
    now_grown = grown[: fields * 3].reshape((fields, 3) + grown.shape[1:])
    prev_grown = grown[fields * 3 : fields * 6].reshape((fields, 3) + grown.shape[1:])
    lame_grown = zpad(grown[fields * 6])
    shear_grown = zpad(grown[fields * 6 + 1])
    buoy_grown = grown[fields * 6 + 2]

    cells = jnp.concatenate([master_cell, receiver_cell])
    amps = [
        jnp.concatenate(
            [
                pick(master_trace[None], master_lag + instant),
                pick(receiver_trace, receiver_lag + instant),
            ]
        )
        for instant in range(STEPS)
    ]
    masks_wide = locate(
        cells, start_x - 1, start_y - 1, width_y, depth, cells_x + 2, cells_y + 2
    )
    masks = masks_wide[:, 1:-1, 1:-1]

    force0, strain0 = stencil(zpad(now_grown), lame_grown, shear_grown)
    now_wide = now_grown[:, :, 1:-1, 1:-1]
    next_wide = advance(
        now_wide,
        prev_grown[:, :, 1:-1, 1:-1],
        force0,
        amps[0],
        masks_wide,
        buoy_grown[1:-1, 1:-1],
    )
    strain0 = strain0[:, :, 1:-1, 1:-1]

    force1, strain1 = stencil(
        zpad(next_wide[1:]), lame_grown[1:-1, 1:-1], shear_grown[1:-1, 1:-1]
    )
    master1 = stencil(zpad(next_wide[:1]), lame_grown[1:-1, 1:-1], shear_grown[1:-1, 1:-1])[1]
    final = advance(
        next_wide[1:, :, 1:-1, 1:-1],
        now_wide[1:, :, 1:-1, 1:-1],
        force1,
        amps[1][1:],
        masks[1:],
        buoy_grown[2:-2, 2:-2],
    )

    weights = jnp.array([1.0, 1.0, 1.0, 2.0, 2.0, 2.0], jnp.float32)[:, None, None, None]
    totals = jnp.zeros((2,) + grid, jnp.float32)
    for master, strain in ((strain0[0], strain0[1:]), (master1[0], strain1)):
        summed = jnp.sum(strain, axis=0)
        dilation_term = (master[0] + master[1] + master[2]) * (summed[0] + summed[1] + summed[2])
        shear_term = 2.0 * jnp.sum(weights * master * summed, axis=0)
        totals = totals + jnp.stack([dilation_term, shear_term])
    totals = totals * (1.0 / (STEPS * receivers * groups))

    share = depth // groups
    gathered = lax.all_to_all(totals, "grp", 3, 0, tiled=True)
    kernels = jnp.sum(gathered.reshape((groups, 2, cells_x, cells_y, share)), axis=0)
    return (final, kernels)


def solution(mesh):
    in_specs = (
        P(None, "gx", "gy", None),
        P(None, "gx", "gy", None),
        P("grp", None, "gx", "gy", None),
        P("grp", None, "gx", "gy", None),
        P("gx", "gy", None),
        P("gx", "gy", None),
        P("gx", "gy", None),
        P(),
        P(),
        P(),
        P("grp"),
        P("grp"),
        P("grp", None, None),
    )
    out_specs = (P("grp", None, "gx", "gy", None), P(None, "gx", "gy", "grp"))
    return jax.shard_map(local, mesh=mesh, in_specs=in_specs, out_specs=out_specs, check_vma=False)
```

```python
import jax
import jax.numpy as jnp
from jax import lax
from jax.sharding import PartitionSpec as P

STEPS = 2


time_step_sq = 0.0625


def with_halo(cells, sides, width):
    for axis, dim in sides:
        count = lax.axis_size(axis)
        ends = count - 1
        head = lax.slice_in_dim(cells, 0, width, axis=dim)
        tail = lax.slice_in_dim(cells, cells.shape[dim] - width, cells.shape[dim], axis=dim)
        cells = jnp.concatenate(
            [
                lax.ppermute(tail, axis, [(i, i + 1) for i in range(ends)]),
                cells,
                lax.ppermute(head, axis, [(i + 1, i) for i in range(ends)]),
            ],
            axis=dim,
        )
    return cells


def backward_diff(stress, axis):
    upper = stress[:, 1:, 1:, 1:]
    if axis == 1:
        lower = stress[:, :-1, 1:, 1:]
    elif axis == 2:
        lower = stress[:, 1:, :-1, 1:]
    else:
        lower = stress[:, 1:, 1:, :-1]
    return upper - lower


def strains_of(padded):
    span_x = padded.shape[2] - 2
    span_y = padded.shape[3] - 2
    span_z = padded.shape[4] - 2
    anchor = padded[:, :, : span_x + 1, : span_y + 1, : span_z + 1]
    grad_x = padded[:, :, 1:, : span_y + 1, : span_z + 1] - anchor
    grad_y = padded[:, :, : span_x + 1, 1:, : span_z + 1] - anchor
    grad_z = padded[:, :, : span_x + 1, : span_y + 1, 1:] - anchor
    strain_xx = grad_x[:, 0]
    strain_yy = grad_y[:, 1]
    strain_zz = grad_z[:, 2]
    strain_xy = 0.5 * (grad_y[:, 0] + grad_x[:, 1])
    strain_xz = 0.5 * (grad_z[:, 0] + grad_x[:, 2])
    strain_yz = 0.5 * (grad_z[:, 1] + grad_y[:, 2])
    return strain_xx, strain_yy, strain_zz, strain_xy, strain_xz, strain_yz


def stencil(padded, lame_pad, shear_pad):
    span_x = padded.shape[2] - 2
    span_y = padded.shape[3] - 2
    span_z = padded.shape[4] - 2
    strain_xx, strain_yy, strain_zz, strain_xy, strain_xz, strain_yz = strains_of(padded)
    lame = lame_pad[: span_x + 1, : span_y + 1, : span_z + 1]
    shear = shear_pad[: span_x + 1, : span_y + 1, : span_z + 1]
    dilation = strain_xx + strain_yy + strain_zz
    stress_xx = lame * dilation + 2.0 * shear * strain_xx
    stress_yy = lame * dilation + 2.0 * shear * strain_yy
    stress_zz = lame * dilation + 2.0 * shear * strain_zz
    stress_xy = 2.0 * shear * strain_xy
    stress_xz = 2.0 * shear * strain_xz
    stress_yz = 2.0 * shear * strain_yz
    force_x = (
        backward_diff(stress_xx, 1) + backward_diff(stress_xy, 2) + backward_diff(stress_xz, 3)
    )
    force_y = (
        backward_diff(stress_xy, 1) + backward_diff(stress_yy, 2) + backward_diff(stress_yz, 3)
    )
    force_z = (
        backward_diff(stress_xz, 1) + backward_diff(stress_yz, 2) + backward_diff(stress_zz, 3)
    )
    force = jnp.stack([force_x, force_y, force_z], axis=1)
    strain = jnp.stack([strain_xx, strain_yy, strain_zz, strain_xy, strain_xz, strain_yz], axis=1)
    return (force, strain[:, :, 1:, 1:, 1:])


def zpad(cells):
    widths = [(0, 0)] * (cells.ndim - 1) + [(1, 1)]
    return jnp.pad(cells, widths)


def locate(cells, start_x, start_y, width_y, depth, span_x, span_y):
    coord_x = cells // (width_y * depth) - start_x
    coord_y = cells // depth % width_y - start_y
    coord_z = cells % depth
    index_x = lax.broadcasted_iota(jnp.int32, (1, span_x, 1, 1), 1)
    index_y = lax.broadcasted_iota(jnp.int32, (1, 1, span_y, 1), 2)
    index_z = lax.broadcasted_iota(jnp.int32, (1, 1, 1, depth), 3)
    found = (
        (index_x == coord_x[:, None, None, None])
        & (index_y == coord_y[:, None, None, None])
        & (index_z == coord_z[:, None, None, None])
    )
    return found.astype(jnp.float32)


def pick(trace, lags):
    positions = lax.broadcasted_iota(jnp.int32, (1, trace.shape[1]), 1)
    chosen = positions == lags[:, None]
    return jnp.sum(jnp.where(chosen[:, :, None], trace, 0.0), axis=1)


def advance(current, earlier, force, amplitudes, masks, buoyancy):
    source = amplitudes[:, :, None, None, None] * masks[:, None]
    return 2.0 * current - earlier + time_step_sq * buoyancy * (force + source)


def exchange_x(stacked, pairs_lo, pairs_hi):
    channels, cells_x, cells_y, depth = stacked.shape
    plane = (cells_y, depth)
    count = lax.axis_size("gx")
    wide_lo = stacked[:pairs_lo, cells_x - 2 :].reshape((-1,) + plane)
    thin_lo = stacked[pairs_lo:, cells_x - 1 :].reshape((-1,) + plane)
    wide_hi = stacked[:pairs_hi, :2].reshape((-1,) + plane)
    thin_hi = stacked[pairs_hi:, :1].reshape((-1,) + plane)
    from_lo = lax.ppermute(
        jnp.concatenate([wide_lo, thin_lo]), "gx", [(i, i + 1) for i in range(count - 1)]
    )
    from_hi = lax.ppermute(
        jnp.concatenate([wide_hi, thin_hi]), "gx", [(i + 1, i) for i in range(count - 1)]
    )
    blank = jnp.zeros((channels - pairs_lo, 1) + plane, jnp.float32)
    rows_lo = jnp.concatenate(
        [
            from_lo[: pairs_lo * 2].reshape((pairs_lo, 2) + plane),
            jnp.concatenate([blank, from_lo[pairs_lo * 2 :].reshape((-1, 1) + plane)], axis=1),
        ]
    )
    blank = jnp.zeros((channels - pairs_hi, 1) + plane, jnp.float32)
    rows_hi = jnp.concatenate(
        [
            from_hi[: pairs_hi * 2].reshape((pairs_hi, 2) + plane),
            jnp.concatenate([from_hi[pairs_hi * 2 :].reshape((-1, 1) + plane), blank], axis=1),
        ]
    )
    return jnp.concatenate([rows_lo, stacked, rows_hi], axis=1)


def local(
    fwd_now,
    fwd_prev,
    adj_now,
    adj_prev,
    lame_first,
    shear_mod,
    buoyancy,
    master_cell,
    master_lag,
    master_trace,
    receiver_cell,
    receiver_lag,
    receiver_trace,
):
    cells_x, cells_y, depth = lame_first.shape
    groups = lax.axis_size("grp")
    receivers = adj_now.shape[0]
    fields = receivers + 1
    width_y = cells_y * lax.axis_size("gy")
    start_x = lax.axis_index("gx") * cells_x
    start_y = lax.axis_index("gy") * cells_y
    grid = (cells_x, cells_y, depth)

    now = jnp.concatenate([fwd_now[None], adj_now]).reshape((fields * 3,) + grid)
    prev = jnp.concatenate([fwd_prev[None], adj_prev]).reshape((fields * 3,) + grid)
    comps = fields * 3
    stacked = jnp.concatenate([now, lame_first[None], shear_mod[None], prev, buoyancy[None]])
    grown = with_halo(exchange_x(stacked, comps + 2, comps), (("gy", 2),), 2)
    now_grown = grown[:comps].reshape((fields, 3) + grown.shape[1:])
    lame_grown = zpad(grown[comps])
    shear_grown = zpad(grown[comps + 1])
    prev_grown = grown[comps + 2 : 2 * comps + 2].reshape((fields, 3) + grown.shape[1:])
    buoy_grown = grown[2 * comps + 2]

    cells = jnp.concatenate([master_cell, receiver_cell])
    amps = [
        jnp.concatenate(
            [
                pick(master_trace[None], master_lag + instant),
                pick(receiver_trace, receiver_lag + instant),
            ]
        )
        for instant in range(STEPS)
    ]
    masks_wide = locate(
        cells, start_x - 1, start_y - 1, width_y, depth, cells_x + 2, cells_y + 2
    )
    masks = masks_wide[:, 1:-1, 1:-1]

    force0, strain0 = stencil(zpad(now_grown), lame_grown, shear_grown)
    now_wide = now_grown[:, :, 1:-1, 1:-1]
    next_wide = advance(
        now_wide,
        prev_grown[:, :, 1:-1, 1:-1],
        force0,
        amps[0],
        masks_wide,
        buoy_grown[1:-1, 1:-1],
    )
    strain0 = strain0[:, :, 1:-1, 1:-1]

    force1, strain1 = stencil(
        zpad(next_wide[1:]), lame_grown[1:-1, 1:-1], shear_grown[1:-1, 1:-1]
    )
    master1 = stencil(zpad(next_wide[:1]), lame_grown[1:-1, 1:-1], shear_grown[1:-1, 1:-1])[1]
    final = advance(
        next_wide[1:, :, 1:-1, 1:-1],
        now_wide[1:, :, 1:-1, 1:-1],
        force1,
        amps[1][1:],
        masks[1:],
        buoy_grown[2:-2, 2:-2],
    )

    weights = jnp.array([1.0, 1.0, 1.0, 2.0, 2.0, 2.0], jnp.float32)[:, None, None, None]
    totals = jnp.zeros((2,) + grid, jnp.float32)
    for master, strain in ((strain0[0], strain0[1:]), (master1[0], strain1)):
        summed = jnp.sum(strain, axis=0)
        dilation_term = (master[0] + master[1] + master[2]) * (summed[0] + summed[1] + summed[2])
        shear_term = 2.0 * jnp.sum(weights * master * summed, axis=0)
        totals = totals + jnp.stack([dilation_term, shear_term])
    totals = totals * (1.0 / (STEPS * receivers * groups))

    share = depth // groups
    gathered = lax.all_to_all(totals, "grp", 3, 0, tiled=True)
    kernels = jnp.sum(gathered.reshape((groups, 2, cells_x, cells_y, share)), axis=0)
    return (final, kernels)


def solution(mesh):
    in_specs = (
        P(None, "gx", "gy", None),
        P(None, "gx", "gy", None),
        P("grp", None, "gx", "gy", None),
        P("grp", None, "gx", "gy", None),
        P("gx", "gy", None),
        P("gx", "gy", None),
        P("gx", "gy", None),
        P(),
        P(),
        P(),
        P("grp"),
        P("grp"),
        P("grp", None, None),
    )
    out_specs = (P("grp", None, "gx", "gy", None), P(None, "gx", "gy", "grp"))
    return jax.shard_map(local, mesh=mesh, in_specs=in_specs, out_specs=out_specs, check_vma=False)
```

```python
import jax
import jax.numpy as jnp
from jax import lax
from jax.sharding import PartitionSpec as P

STEPS = 2


time_step_sq = 0.0625


def with_halo(cells, sides, width):
    for axis, dim in sides:
        count = lax.axis_size(axis)
        ends = count - 1
        head = lax.slice_in_dim(cells, 0, width, axis=dim)
        tail = lax.slice_in_dim(cells, cells.shape[dim] - width, cells.shape[dim], axis=dim)
        cells = jnp.concatenate(
            [
                lax.ppermute(tail, axis, [(i, i + 1) for i in range(ends)]),
                cells,
                lax.ppermute(head, axis, [(i + 1, i) for i in range(ends)]),
            ],
            axis=dim,
        )
    return cells


def backward_diff(stress, axis):
    upper = stress[:, 1:, 1:, 1:]
    if axis == 1:
        lower = stress[:, :-1, 1:, 1:]
    elif axis == 2:
        lower = stress[:, 1:, :-1, 1:]
    else:
        lower = stress[:, 1:, 1:, :-1]
    return upper - lower


def strains_of(padded):
    span_x = padded.shape[2] - 2
    span_y = padded.shape[3] - 2
    span_z = padded.shape[4] - 2
    anchor = padded[:, :, : span_x + 1, : span_y + 1, : span_z + 1]
    grad_x = padded[:, :, 1:, : span_y + 1, : span_z + 1] - anchor
    grad_y = padded[:, :, : span_x + 1, 1:, : span_z + 1] - anchor
    grad_z = padded[:, :, : span_x + 1, : span_y + 1, 1:] - anchor
    strain_xx = grad_x[:, 0]
    strain_yy = grad_y[:, 1]
    strain_zz = grad_z[:, 2]
    strain_xy = 0.5 * (grad_y[:, 0] + grad_x[:, 1])
    strain_xz = 0.5 * (grad_z[:, 0] + grad_x[:, 2])
    strain_yz = 0.5 * (grad_z[:, 1] + grad_y[:, 2])
    return strain_xx, strain_yy, strain_zz, strain_xy, strain_xz, strain_yz


def stencil(padded, lame_pad, shear_pad):
    span_x = padded.shape[2] - 2
    span_y = padded.shape[3] - 2
    span_z = padded.shape[4] - 2
    strain_xx, strain_yy, strain_zz, strain_xy, strain_xz, strain_yz = strains_of(padded)
    lame = lame_pad[: span_x + 1, : span_y + 1, : span_z + 1]
    shear = shear_pad[: span_x + 1, : span_y + 1, : span_z + 1]
    dilation = strain_xx + strain_yy + strain_zz
    stress_xx = lame * dilation + 2.0 * shear * strain_xx
    stress_yy = lame * dilation + 2.0 * shear * strain_yy
    stress_zz = lame * dilation + 2.0 * shear * strain_zz
    stress_xy = 2.0 * shear * strain_xy
    stress_xz = 2.0 * shear * strain_xz
    stress_yz = 2.0 * shear * strain_yz
    force_x = (
        backward_diff(stress_xx, 1) + backward_diff(stress_xy, 2) + backward_diff(stress_xz, 3)
    )
    force_y = (
        backward_diff(stress_xy, 1) + backward_diff(stress_yy, 2) + backward_diff(stress_yz, 3)
    )
    force_z = (
        backward_diff(stress_xz, 1) + backward_diff(stress_yz, 2) + backward_diff(stress_zz, 3)
    )
    force = jnp.stack([force_x, force_y, force_z], axis=1)
    strain = jnp.stack([strain_xx, strain_yy, strain_zz, strain_xy, strain_xz, strain_yz], axis=1)
    return (force, strain[:, :, 1:, 1:, 1:])


def zpad(cells):
    widths = [(0, 0)] * (cells.ndim - 1) + [(1, 1)]
    return jnp.pad(cells, widths)


def locate(cells, start_x, start_y, width_y, depth, span_x, span_y):
    coord_x = cells // (width_y * depth) - start_x
    coord_y = cells // depth % width_y - start_y
    coord_z = cells % depth
    index_x = lax.broadcasted_iota(jnp.int32, (1, span_x, 1, 1), 1)
    index_y = lax.broadcasted_iota(jnp.int32, (1, 1, span_y, 1), 2)
    index_z = lax.broadcasted_iota(jnp.int32, (1, 1, 1, depth), 3)
    found = (
        (index_x == coord_x[:, None, None, None])
        & (index_y == coord_y[:, None, None, None])
        & (index_z == coord_z[:, None, None, None])
    )
    return found.astype(jnp.float32)


def pick(trace, lags):
    positions = lax.broadcasted_iota(jnp.int32, (1, trace.shape[1]), 1)
    chosen = positions == lags[:, None]
    return jnp.sum(jnp.where(chosen[:, :, None], trace, 0.0), axis=1)


def advance(current, earlier, force, amplitudes, masks, buoyancy):
    source = amplitudes[:, :, None, None, None] * masks[:, None]
    return 2.0 * current - earlier + time_step_sq * buoyancy * (force + source)


def exchange_x(stacked, pairs_lo, pairs_hi):
    channels, cells_x, cells_y, depth = stacked.shape
    plane = (cells_y, depth)
    count = lax.axis_size("gx")
    wide_lo = stacked[:pairs_lo, cells_x - 2 :].reshape((-1,) + plane)
    thin_lo = stacked[pairs_lo:, cells_x - 1 :].reshape((-1,) + plane)
    wide_hi = stacked[:pairs_hi, :2].reshape((-1,) + plane)
    thin_hi = stacked[pairs_hi:, :1].reshape((-1,) + plane)
    from_lo = lax.ppermute(
        jnp.concatenate([wide_lo, thin_lo]), "gx", [(i, i + 1) for i in range(count - 1)]
    )
    from_hi = lax.ppermute(
        jnp.concatenate([wide_hi, thin_hi]), "gx", [(i + 1, i) for i in range(count - 1)]
    )
    blank = jnp.zeros((channels - pairs_lo, 1) + plane, jnp.float32)
    rows_lo = jnp.concatenate(
        [
            from_lo[: pairs_lo * 2].reshape((pairs_lo, 2) + plane),
            jnp.concatenate([blank, from_lo[pairs_lo * 2 :].reshape((-1, 1) + plane)], axis=1),
        ]
    )
    blank = jnp.zeros((channels - pairs_hi, 1) + plane, jnp.float32)
    rows_hi = jnp.concatenate(
        [
            from_hi[: pairs_hi * 2].reshape((pairs_hi, 2) + plane),
            jnp.concatenate([from_hi[pairs_hi * 2 :].reshape((-1, 1) + plane), blank], axis=1),
        ]
    )
    return jnp.concatenate([rows_lo, stacked, rows_hi], axis=1)


def up_z(cells):
    top = lax.broadcasted_iota(jnp.int32, cells.shape, cells.ndim - 1) == cells.shape[-1] - 1
    return jnp.where(top, 0.0, jnp.roll(cells, -1, axis=-1))


def down_z(cells):
    bottom = lax.broadcasted_iota(jnp.int32, cells.shape, cells.ndim - 1) == 0
    return jnp.where(bottom, 0.0, jnp.roll(cells, 1, axis=-1))


def dense_stencil(cells, lame, shear):
    lower = cells[:, :, :-1]
    grad_x = cells[:, :, 1:] - lower
    grad_y = jnp.roll(lower, -1, axis=3) - lower
    grad_z = up_z(lower) - lower
    strain_xx = grad_x[:, 0]
    strain_yy = grad_y[:, 1]
    strain_zz = grad_z[:, 2]
    strain_xy = 0.5 * (grad_y[:, 0] + grad_x[:, 1])
    strain_xz = 0.5 * (grad_z[:, 0] + grad_x[:, 2])
    strain_yz = 0.5 * (grad_z[:, 1] + grad_y[:, 2])
    lame = lame[:-1]
    shear = shear[:-1]
    dilation = strain_xx + strain_yy + strain_zz
    stress_xx = lame * dilation + 2.0 * shear * strain_xx
    stress_yy = lame * dilation + 2.0 * shear * strain_yy
    stress_zz = lame * dilation + 2.0 * shear * strain_zz
    stress_xy = 2.0 * shear * strain_xy
    stress_xz = 2.0 * shear * strain_xz
    stress_yz = 2.0 * shear * strain_yz

    def diff_x(stress):
        return stress[:, 1:] - stress[:, :-1]

    def diff_y(stress):
        return (stress - jnp.roll(stress, 1, axis=2))[:, 1:]

    def diff_z(stress):
        return (stress - down_z(stress))[:, 1:]

    force_x = diff_x(stress_xx) + diff_y(stress_xy) + diff_z(stress_xz)
    force_y = diff_x(stress_xy) + diff_y(stress_yy) + diff_z(stress_yz)
    force_z = diff_x(stress_xz) + diff_y(stress_yz) + diff_z(stress_zz)
    force = jnp.stack([force_x, force_y, force_z], axis=1)
    strain = jnp.stack([strain_xx, strain_yy, strain_zz, strain_xy, strain_xz, strain_yz], axis=1)
    return (force, strain)


def local(
    fwd_now,
    fwd_prev,
    adj_now,
    adj_prev,
    lame_first,
    shear_mod,
    buoyancy,
    master_cell,
    master_lag,
    master_trace,
    receiver_cell,
    receiver_lag,
    receiver_trace,
):
    cells_x, cells_y, depth = lame_first.shape
    groups = lax.axis_size("grp")
    receivers = adj_now.shape[0]
    fields = receivers + 1
    width_y = cells_y * lax.axis_size("gy")
    start_x = lax.axis_index("gx") * cells_x
    start_y = lax.axis_index("gy") * cells_y
    grid = (cells_x, cells_y, depth)

    now = jnp.concatenate([fwd_now[None], adj_now]).reshape((fields * 3,) + grid)
    prev = jnp.concatenate([fwd_prev[None], adj_prev]).reshape((fields * 3,) + grid)
    comps = fields * 3
    stacked = jnp.concatenate([now, lame_first[None], shear_mod[None], prev, buoyancy[None]])
    grown = with_halo(exchange_x(stacked, comps + 2, comps), (("gy", 2),), 2)
    span_y = 16 * ((cells_y + 4 + 15) // 16)
    grown = jnp.pad(grown, ((0, 0), (0, 0), (0, span_y - cells_y - 4), (0, 0)))
    now_grown = grown[:comps].reshape((fields, 3) + grown.shape[1:])
    lame_grown = grown[comps]
    shear_grown = grown[comps + 1]
    prev_grown = grown[comps + 2 : 2 * comps + 2].reshape((fields, 3) + grown.shape[1:])
    buoy_grown = grown[2 * comps + 2]

    cells = jnp.concatenate([master_cell, receiver_cell])
    amps = [
        jnp.concatenate(
            [
                pick(master_trace[None], master_lag + instant),
                pick(receiver_trace, receiver_lag + instant),
            ]
        )
        for instant in range(STEPS)
    ]
    masks_wide = locate(cells, start_x - 1, start_y - 2, width_y, depth, cells_x + 2, span_y)
    inner = (slice(None), slice(1, 1 + cells_x), slice(2, 2 + cells_y))

    force0, strain0 = dense_stencil(now_grown, lame_grown, shear_grown)
    now_wide = now_grown[:, :, 1:-1]
    next_wide = advance(
        now_wide,
        prev_grown[:, :, 1:-1],
        force0,
        amps[0],
        masks_wide,
        buoy_grown[1:-1],
    )
    strain0 = strain0[:, :, 2 : 2 + cells_x, 2 : 2 + cells_y]

    force1, strain1 = dense_stencil(next_wide[1:], lame_grown[1:-1], shear_grown[1:-1])
    master1 = dense_stencil(next_wide[:1], lame_grown[1:-1], shear_grown[1:-1])[1]
    strain1 = strain1[:, :, 1 : 1 + cells_x, 2 : 2 + cells_y]
    master1 = master1[:, :, 1 : 1 + cells_x, 2 : 2 + cells_y]
    final = advance(
        next_wide[1:, :, 1 : 1 + cells_x],
        now_wide[1:, :, 1 : 1 + cells_x],
        force1,
        amps[1][1:],
        masks_wide[1:, 1 : 1 + cells_x],
        buoy_grown[2 : 2 + cells_x],
    )[:, :, :, 2 : 2 + cells_y]

    weights = jnp.array([1.0, 1.0, 1.0, 2.0, 2.0, 2.0], jnp.float32)[:, None, None, None]
    totals = jnp.zeros((2,) + grid, jnp.float32)
    for master, strain in ((strain0[0], strain0[1:]), (master1[0], strain1)):
        summed = jnp.sum(strain, axis=0)
        dilation_term = (master[0] + master[1] + master[2]) * (summed[0] + summed[1] + summed[2])
        shear_term = 2.0 * jnp.sum(weights * master * summed, axis=0)
        totals = totals + jnp.stack([dilation_term, shear_term])
    totals = totals * (1.0 / (STEPS * receivers * groups))

    share = depth // groups
    gathered = lax.all_to_all(totals, "grp", 3, 0, tiled=True)
    kernels = jnp.sum(gathered.reshape((groups, 2, cells_x, cells_y, share)), axis=0)
    return (final, kernels)


def solution(mesh):
    in_specs = (
        P(None, "gx", "gy", None),
        P(None, "gx", "gy", None),
        P("grp", None, "gx", "gy", None),
        P("grp", None, "gx", "gy", None),
        P("gx", "gy", None),
        P("gx", "gy", None),
        P("gx", "gy", None),
        P(),
        P(),
        P(),
        P("grp"),
        P("grp"),
        P("grp", None, None),
    )
    out_specs = (P("grp", None, "gx", "gy", None), P(None, "gx", "gy", "grp"))
    return jax.shard_map(local, mesh=mesh, in_specs=in_specs, out_specs=out_specs, check_vma=False)
```

```python
import jax
import jax.numpy as jnp
from jax import lax
from jax.sharding import PartitionSpec as P

STEPS = 2


time_step_sq = 0.0625


def with_halo(cells, sides, width):
    for axis, dim in sides:
        count = lax.axis_size(axis)
        ends = count - 1
        head = lax.slice_in_dim(cells, 0, width, axis=dim)
        tail = lax.slice_in_dim(cells, cells.shape[dim] - width, cells.shape[dim], axis=dim)
        cells = jnp.concatenate(
            [
                lax.ppermute(tail, axis, [(i, i + 1) for i in range(ends)]),
                cells,
                lax.ppermute(head, axis, [(i + 1, i) for i in range(ends)]),
            ],
            axis=dim,
        )
    return cells


def backward_diff(stress, axis):
    upper = stress[:, 1:, 1:, 1:]
    if axis == 1:
        lower = stress[:, :-1, 1:, 1:]
    elif axis == 2:
        lower = stress[:, 1:, :-1, 1:]
    else:
        lower = stress[:, 1:, 1:, :-1]
    return upper - lower


def strains_of(padded):
    span_x = padded.shape[2] - 2
    span_y = padded.shape[3] - 2
    span_z = padded.shape[4] - 2
    anchor = padded[:, :, : span_x + 1, : span_y + 1, : span_z + 1]
    grad_x = padded[:, :, 1:, : span_y + 1, : span_z + 1] - anchor
    grad_y = padded[:, :, : span_x + 1, 1:, : span_z + 1] - anchor
    grad_z = padded[:, :, : span_x + 1, : span_y + 1, 1:] - anchor
    strain_xx = grad_x[:, 0]
    strain_yy = grad_y[:, 1]
    strain_zz = grad_z[:, 2]
    strain_xy = 0.5 * (grad_y[:, 0] + grad_x[:, 1])
    strain_xz = 0.5 * (grad_z[:, 0] + grad_x[:, 2])
    strain_yz = 0.5 * (grad_z[:, 1] + grad_y[:, 2])
    return strain_xx, strain_yy, strain_zz, strain_xy, strain_xz, strain_yz


def stencil(padded, lame_pad, shear_pad):
    span_x = padded.shape[2] - 2
    span_y = padded.shape[3] - 2
    span_z = padded.shape[4] - 2
    strain_xx, strain_yy, strain_zz, strain_xy, strain_xz, strain_yz = strains_of(padded)
    lame = lame_pad[: span_x + 1, : span_y + 1, : span_z + 1]
    shear = shear_pad[: span_x + 1, : span_y + 1, : span_z + 1]
    dilation = strain_xx + strain_yy + strain_zz
    stress_xx = lame * dilation + 2.0 * shear * strain_xx
    stress_yy = lame * dilation + 2.0 * shear * strain_yy
    stress_zz = lame * dilation + 2.0 * shear * strain_zz
    stress_xy = 2.0 * shear * strain_xy
    stress_xz = 2.0 * shear * strain_xz
    stress_yz = 2.0 * shear * strain_yz
    force_x = (
        backward_diff(stress_xx, 1) + backward_diff(stress_xy, 2) + backward_diff(stress_xz, 3)
    )
    force_y = (
        backward_diff(stress_xy, 1) + backward_diff(stress_yy, 2) + backward_diff(stress_yz, 3)
    )
    force_z = (
        backward_diff(stress_xz, 1) + backward_diff(stress_yz, 2) + backward_diff(stress_zz, 3)
    )
    force = jnp.stack([force_x, force_y, force_z], axis=1)
    strain = jnp.stack([strain_xx, strain_yy, strain_zz, strain_xy, strain_xz, strain_yz], axis=1)
    return (force, strain[:, :, 1:, 1:, 1:])


def zpad(cells):
    widths = [(0, 0)] * (cells.ndim - 1) + [(1, 1)]
    return jnp.pad(cells, widths)


def locate(cells, start_x, start_y, width_y, depth, span_x, span_y):
    coord_x = cells // (width_y * depth) - start_x
    coord_y = cells // depth % width_y - start_y
    coord_z = cells % depth
    index_x = lax.broadcasted_iota(jnp.int32, (1, span_x, 1, 1), 1)
    index_y = lax.broadcasted_iota(jnp.int32, (1, 1, span_y, 1), 2)
    index_z = lax.broadcasted_iota(jnp.int32, (1, 1, 1, depth), 3)
    found = (
        (index_x == coord_x[:, None, None, None])
        & (index_y == coord_y[:, None, None, None])
        & (index_z == coord_z[:, None, None, None])
    )
    return found.astype(jnp.float32)


def pick(trace, lags):
    positions = lax.broadcasted_iota(jnp.int32, (1, trace.shape[1]), 1)
    chosen = positions == lags[:, None]
    return jnp.sum(jnp.where(chosen[:, :, None], trace, 0.0), axis=1)


def advance(current, earlier, force, amplitudes, masks, buoyancy):
    source = amplitudes[:, :, None, None, None] * masks[:, None]
    return 2.0 * current - earlier + time_step_sq * buoyancy * (force + source)


def exchange_x(stacked, send_lo, send_hi, pairs_lo, pairs_hi):
    channels, cells_x, cells_y, depth = stacked.shape
    plane = (cells_y, depth)
    count = lax.axis_size("gx")
    from_lo = lax.ppermute(send_lo, "gx", [(i, i + 1) for i in range(count - 1)])
    from_hi = lax.ppermute(send_hi, "gx", [(i + 1, i) for i in range(count - 1)])
    blank = jnp.zeros((channels - pairs_lo, 1) + plane, jnp.float32)
    rows_lo = jnp.concatenate(
        [
            from_lo[: pairs_lo * 2].reshape((pairs_lo, 2) + plane),
            jnp.concatenate([blank, from_lo[pairs_lo * 2 :].reshape((-1, 1) + plane)], axis=1),
        ]
    )
    blank = jnp.zeros((channels - pairs_hi, 1) + plane, jnp.float32)
    rows_hi = jnp.concatenate(
        [
            from_hi[: pairs_hi * 2].reshape((pairs_hi, 2) + plane),
            jnp.concatenate([from_hi[pairs_hi * 2 :].reshape((-1, 1) + plane), blank], axis=1),
        ]
    )
    return jnp.concatenate([rows_lo, stacked, rows_hi], axis=1)


def up_z(cells):
    top = lax.broadcasted_iota(jnp.int32, cells.shape, cells.ndim - 1) == cells.shape[-1] - 1
    return jnp.where(top, 0.0, jnp.roll(cells, -1, axis=-1))


def down_z(cells):
    bottom = lax.broadcasted_iota(jnp.int32, cells.shape, cells.ndim - 1) == 0
    return jnp.where(bottom, 0.0, jnp.roll(cells, 1, axis=-1))


def dense_stencil(cells, lame, shear):
    lower = cells[:, :, :-1]
    grad_x = cells[:, :, 1:] - lower
    grad_y = jnp.roll(lower, -1, axis=3) - lower
    grad_z = up_z(lower) - lower
    strain_xx = grad_x[:, 0]
    strain_yy = grad_y[:, 1]
    strain_zz = grad_z[:, 2]
    strain_xy = 0.5 * (grad_y[:, 0] + grad_x[:, 1])
    strain_xz = 0.5 * (grad_z[:, 0] + grad_x[:, 2])
    strain_yz = 0.5 * (grad_z[:, 1] + grad_y[:, 2])
    lame = lame[:-1]
    shear = shear[:-1]
    dilation = strain_xx + strain_yy + strain_zz
    stress_xx = lame * dilation + 2.0 * shear * strain_xx
    stress_yy = lame * dilation + 2.0 * shear * strain_yy
    stress_zz = lame * dilation + 2.0 * shear * strain_zz
    stress_xy = 2.0 * shear * strain_xy
    stress_xz = 2.0 * shear * strain_xz
    stress_yz = 2.0 * shear * strain_yz

    def diff_x(stress):
        return stress[:, 1:] - stress[:, :-1]

    def diff_y(stress):
        return (stress - jnp.roll(stress, 1, axis=2))[:, 1:]

    def diff_z(stress):
        return (stress - down_z(stress))[:, 1:]

    force_x = diff_x(stress_xx) + diff_y(stress_xy) + diff_z(stress_xz)
    force_y = diff_x(stress_xy) + diff_y(stress_yy) + diff_z(stress_yz)
    force_z = diff_x(stress_xz) + diff_y(stress_yz) + diff_z(stress_zz)
    force = jnp.stack([force_x, force_y, force_z], axis=1)
    strain = jnp.stack([strain_xx, strain_yy, strain_zz, strain_xy, strain_xz, strain_yz], axis=1)
    return (force, strain)


def local(
    fwd_now,
    fwd_prev,
    adj_now,
    adj_prev,
    lame_first,
    shear_mod,
    buoyancy,
    master_cell,
    master_lag,
    master_trace,
    receiver_cell,
    receiver_lag,
    receiver_trace,
):
    cells_x, cells_y, depth = lame_first.shape
    groups = lax.axis_size("grp")
    receivers = adj_now.shape[0]
    fields = receivers + 1
    width_y = cells_y * lax.axis_size("gy")
    start_x = lax.axis_index("gx") * cells_x
    start_y = lax.axis_index("gy") * cells_y
    grid = (cells_x, cells_y, depth)

    now = jnp.concatenate([fwd_now[None], adj_now]).reshape((fields * 3,) + grid)
    prev = jnp.concatenate([fwd_prev[None], adj_prev]).reshape((fields * 3,) + grid)
    comps = fields * 3
    stacked = jnp.concatenate([now, lame_first[None], shear_mod[None], prev, buoyancy[None]])
    plane = (cells_y, depth)

    def rows(first, last):
        parts = [
            fwd_now[:, first:last],
            adj_now[:, :, first:last].reshape((receivers * 3, last - first) + plane),
            lame_first[None, first:last],
            shear_mod[None, first:last],
            fwd_prev[:, first:last],
            adj_prev[:, :, first:last].reshape((receivers * 3, last - first) + plane),
            buoyancy[None, first:last],
        ]
        return [part.reshape((-1,) + plane) for part in parts]

    last_two = rows(cells_x - 2, cells_x)
    last_one = rows(cells_x - 1, cells_x)
    first_two = rows(0, 2)
    first_one = rows(0, 1)
    send_lo = jnp.concatenate(last_two[:4] + last_one[4:])
    send_hi = jnp.concatenate(first_two[:2] + first_one[2:])
    grown = exchange_x(stacked, send_lo, send_hi, comps + 2, comps)
    grown = with_halo(grown, (("gy", 2),), 2)
    span_y = 16 * ((cells_y + 4 + 15) // 16)
    grown = jnp.pad(grown, ((0, 0), (0, 0), (0, span_y - cells_y - 4), (0, 0)))
    now_grown = grown[:comps].reshape((fields, 3) + grown.shape[1:])
    lame_grown = grown[comps]
    shear_grown = grown[comps + 1]
    prev_grown = grown[comps + 2 : 2 * comps + 2].reshape((fields, 3) + grown.shape[1:])
    buoy_grown = grown[2 * comps + 2]

    cells = jnp.concatenate([master_cell, receiver_cell])
    amps = [
        jnp.concatenate(
            [
                pick(master_trace[None], master_lag + instant),
                pick(receiver_trace, receiver_lag + instant),
            ]
        )
        for instant in range(STEPS)
    ]
    masks_wide = locate(cells, start_x - 1, start_y - 2, width_y, depth, cells_x + 2, span_y)
    inner = (slice(None), slice(1, 1 + cells_x), slice(2, 2 + cells_y))

    force0, strain0 = dense_stencil(now_grown, lame_grown, shear_grown)
    now_wide = now_grown[:, :, 1:-1]
    next_wide = advance(
        now_wide,
        prev_grown[:, :, 1:-1],
        force0,
        amps[0],
        masks_wide,
        buoy_grown[1:-1],
    )
    strain0 = strain0[:, :, 2 : 2 + cells_x, 2 : 2 + cells_y]

    force1, strain1 = dense_stencil(next_wide[1:], lame_grown[1:-1], shear_grown[1:-1])
    master1 = dense_stencil(next_wide[:1], lame_grown[1:-1], shear_grown[1:-1])[1]
    strain1 = strain1[:, :, 1 : 1 + cells_x, 2 : 2 + cells_y]
    master1 = master1[:, :, 1 : 1 + cells_x, 2 : 2 + cells_y]
    final = advance(
        next_wide[1:, :, 1 : 1 + cells_x],
        now_wide[1:, :, 1 : 1 + cells_x],
        force1,
        amps[1][1:],
        masks_wide[1:, 1 : 1 + cells_x],
        buoy_grown[2 : 2 + cells_x],
    )[:, :, :, 2 : 2 + cells_y]

    weights = jnp.array([1.0, 1.0, 1.0, 2.0, 2.0, 2.0], jnp.float32)[:, None, None, None]
    totals = jnp.zeros((2,) + grid, jnp.float32)
    for master, strain in ((strain0[0], strain0[1:]), (master1[0], strain1)):
        summed = jnp.sum(strain, axis=0)
        dilation_term = (master[0] + master[1] + master[2]) * (summed[0] + summed[1] + summed[2])
        shear_term = 2.0 * jnp.sum(weights * master * summed, axis=0)
        totals = totals + jnp.stack([dilation_term, shear_term])
    totals = totals * (1.0 / (STEPS * receivers * groups))

    share = depth // groups
    gathered = lax.all_to_all(totals, "grp", 3, 0, tiled=True)
    kernels = jnp.sum(gathered.reshape((groups, 2, cells_x, cells_y, share)), axis=0)
    return (final, kernels)


def solution(mesh):
    in_specs = (
        P(None, "gx", "gy", None),
        P(None, "gx", "gy", None),
        P("grp", None, "gx", "gy", None),
        P("grp", None, "gx", "gy", None),
        P("gx", "gy", None),
        P("gx", "gy", None),
        P("gx", "gy", None),
        P(),
        P(),
        P(),
        P("grp"),
        P("grp"),
        P("grp", None, None),
    )
    out_specs = (P("grp", None, "gx", "gy", None), P(None, "gx", "gy", "grp"))
    return jax.shard_map(local, mesh=mesh, in_specs=in_specs, out_specs=out_specs, check_vma=False)
```

```python
import jax
import jax.numpy as jnp
from jax import lax
from jax.sharding import PartitionSpec as P

STEPS = 2


time_step_sq = 0.0625


def with_halo(cells, sides, width):
    for axis, dim in sides:
        count = lax.axis_size(axis)
        ends = count - 1
        head = lax.slice_in_dim(cells, 0, width, axis=dim)
        tail = lax.slice_in_dim(cells, cells.shape[dim] - width, cells.shape[dim], axis=dim)
        cells = jnp.concatenate(
            [
                lax.ppermute(tail, axis, [(i, i + 1) for i in range(ends)]),
                cells,
                lax.ppermute(head, axis, [(i + 1, i) for i in range(ends)]),
            ],
            axis=dim,
        )
    return cells


def backward_diff(stress, axis):
    upper = stress[:, 1:, 1:, 1:]
    if axis == 1:
        lower = stress[:, :-1, 1:, 1:]
    elif axis == 2:
        lower = stress[:, 1:, :-1, 1:]
    else:
        lower = stress[:, 1:, 1:, :-1]
    return upper - lower


def strains_of(padded):
    span_x = padded.shape[2] - 2
    span_y = padded.shape[3] - 2
    span_z = padded.shape[4] - 2
    anchor = padded[:, :, : span_x + 1, : span_y + 1, : span_z + 1]
    grad_x = padded[:, :, 1:, : span_y + 1, : span_z + 1] - anchor
    grad_y = padded[:, :, : span_x + 1, 1:, : span_z + 1] - anchor
    grad_z = padded[:, :, : span_x + 1, : span_y + 1, 1:] - anchor
    strain_xx = grad_x[:, 0]
    strain_yy = grad_y[:, 1]
    strain_zz = grad_z[:, 2]
    strain_xy = 0.5 * (grad_y[:, 0] + grad_x[:, 1])
    strain_xz = 0.5 * (grad_z[:, 0] + grad_x[:, 2])
    strain_yz = 0.5 * (grad_z[:, 1] + grad_y[:, 2])
    return strain_xx, strain_yy, strain_zz, strain_xy, strain_xz, strain_yz


def stencil(padded, lame_pad, shear_pad):
    span_x = padded.shape[2] - 2
    span_y = padded.shape[3] - 2
    span_z = padded.shape[4] - 2
    strain_xx, strain_yy, strain_zz, strain_xy, strain_xz, strain_yz = strains_of(padded)
    lame = lame_pad[: span_x + 1, : span_y + 1, : span_z + 1]
    shear = shear_pad[: span_x + 1, : span_y + 1, : span_z + 1]
    dilation = strain_xx + strain_yy + strain_zz
    stress_xx = lame * dilation + 2.0 * shear * strain_xx
    stress_yy = lame * dilation + 2.0 * shear * strain_yy
    stress_zz = lame * dilation + 2.0 * shear * strain_zz
    stress_xy = 2.0 * shear * strain_xy
    stress_xz = 2.0 * shear * strain_xz
    stress_yz = 2.0 * shear * strain_yz
    force_x = (
        backward_diff(stress_xx, 1) + backward_diff(stress_xy, 2) + backward_diff(stress_xz, 3)
    )
    force_y = (
        backward_diff(stress_xy, 1) + backward_diff(stress_yy, 2) + backward_diff(stress_yz, 3)
    )
    force_z = (
        backward_diff(stress_xz, 1) + backward_diff(stress_yz, 2) + backward_diff(stress_zz, 3)
    )
    force = jnp.stack([force_x, force_y, force_z], axis=1)
    strain = jnp.stack([strain_xx, strain_yy, strain_zz, strain_xy, strain_xz, strain_yz], axis=1)
    return (force, strain[:, :, 1:, 1:, 1:])


def zpad(cells):
    widths = [(0, 0)] * (cells.ndim - 1) + [(1, 1)]
    return jnp.pad(cells, widths)


def locate(cells, start_x, start_y, width_y, depth, span_x, span_y):
    coord_x = cells // (width_y * depth) - start_x
    coord_y = cells // depth % width_y - start_y
    coord_z = cells % depth
    index_x = lax.broadcasted_iota(jnp.int32, (1, span_x, 1, 1), 1)
    index_y = lax.broadcasted_iota(jnp.int32, (1, 1, span_y, 1), 2)
    index_z = lax.broadcasted_iota(jnp.int32, (1, 1, 1, depth), 3)
    found = (
        (index_x == coord_x[:, None, None, None])
        & (index_y == coord_y[:, None, None, None])
        & (index_z == coord_z[:, None, None, None])
    )
    return found.astype(jnp.float32)


def pick(trace, lags):
    positions = lax.broadcasted_iota(jnp.int32, (1, trace.shape[1]), 1)
    chosen = positions == lags[:, None]
    return jnp.sum(jnp.where(chosen[:, :, None], trace, 0.0), axis=1)


def advance(current, earlier, force, amplitudes, masks, buoyancy):
    source = amplitudes[:, :, None, None, None] * masks[:, None]
    return 2.0 * current - earlier + time_step_sq * buoyancy * (force + source)


def exchange_x(stacked, pairs_lo, pairs_hi):
    channels, cells_x, cells_y, depth = stacked.shape
    plane = (cells_y, depth)
    count = lax.axis_size("gx")
    wide_lo = stacked[:pairs_lo, cells_x - 2 :].reshape((-1,) + plane)
    thin_lo = stacked[pairs_lo:, cells_x - 1 :].reshape((-1,) + plane)
    wide_hi = stacked[:pairs_hi, :2].reshape((-1,) + plane)
    thin_hi = stacked[pairs_hi:, :1].reshape((-1,) + plane)
    from_lo = lax.ppermute(
        jnp.concatenate([wide_lo, thin_lo]), "gx", [(i, i + 1) for i in range(count - 1)]
    )
    from_hi = lax.ppermute(
        jnp.concatenate([wide_hi, thin_hi]), "gx", [(i + 1, i) for i in range(count - 1)]
    )
    blank = jnp.zeros((channels - pairs_lo, 1) + plane, jnp.float32)
    rows_lo = jnp.concatenate(
        [
            from_lo[: pairs_lo * 2].reshape((pairs_lo, 2) + plane),
            jnp.concatenate([blank, from_lo[pairs_lo * 2 :].reshape((-1, 1) + plane)], axis=1),
        ]
    )
    blank = jnp.zeros((channels - pairs_hi, 1) + plane, jnp.float32)
    rows_hi = jnp.concatenate(
        [
            from_hi[: pairs_hi * 2].reshape((pairs_hi, 2) + plane),
            jnp.concatenate([from_hi[pairs_hi * 2 :].reshape((-1, 1) + plane), blank], axis=1),
        ]
    )
    return jnp.concatenate([rows_lo, stacked, rows_hi], axis=1)


def up_z(cells):
    top = lax.broadcasted_iota(jnp.int32, cells.shape, cells.ndim - 1) == cells.shape[-1] - 1
    return jnp.where(top, 0.0, jnp.roll(cells, -1, axis=-1))


def down_z(cells):
    bottom = lax.broadcasted_iota(jnp.int32, cells.shape, cells.ndim - 1) == 0
    return jnp.where(bottom, 0.0, jnp.roll(cells, 1, axis=-1))


def dense_stencil(cells, lame, shear):
    lower = cells[:, :, :-1]
    grad_x = cells[:, :, 1:] - lower
    grad_y = jnp.roll(lower, -1, axis=3) - lower
    grad_z = up_z(lower) - lower
    strain_xx = grad_x[:, 0]
    strain_yy = grad_y[:, 1]
    strain_zz = grad_z[:, 2]
    strain_xy = 0.5 * (grad_y[:, 0] + grad_x[:, 1])
    strain_xz = 0.5 * (grad_z[:, 0] + grad_x[:, 2])
    strain_yz = 0.5 * (grad_z[:, 1] + grad_y[:, 2])
    lame = lame[:-1]
    shear = shear[:-1]
    dilation = strain_xx + strain_yy + strain_zz
    stress_xx = lame * dilation + 2.0 * shear * strain_xx
    stress_yy = lame * dilation + 2.0 * shear * strain_yy
    stress_zz = lame * dilation + 2.0 * shear * strain_zz
    stress_xy = 2.0 * shear * strain_xy
    stress_xz = 2.0 * shear * strain_xz
    stress_yz = 2.0 * shear * strain_yz

    def diff_x(stress):
        return stress[:, 1:] - stress[:, :-1]

    def diff_y(stress):
        return (stress - jnp.roll(stress, 1, axis=2))[:, 1:]

    def diff_z(stress):
        return (stress - down_z(stress))[:, 1:]

    force_x = diff_x(stress_xx) + diff_y(stress_xy) + diff_z(stress_xz)
    force_y = diff_x(stress_xy) + diff_y(stress_yy) + diff_z(stress_yz)
    force_z = diff_x(stress_xz) + diff_y(stress_yz) + diff_z(stress_zz)
    force = jnp.stack([force_x, force_y, force_z], axis=1)
    strain = jnp.stack([strain_xx, strain_yy, strain_zz, strain_xy, strain_xz, strain_yz], axis=1)
    return (force, strain)


def exchange_y(grown, pairs_lo, pairs_hi, span_y):
    channels, cells_x, cells_y, depth = grown.shape
    count = lax.axis_size("gy")
    wide_lo = grown[:pairs_lo, :, cells_y - 2 :].reshape((-1, depth))
    thin_lo = grown[pairs_lo:, :, cells_y - 1 :].reshape((-1, depth))
    wide_hi = grown[:pairs_hi, :, :2].reshape((-1, depth))
    thin_hi = grown[pairs_hi:, :, :1].reshape((-1, depth))
    from_lo = lax.ppermute(
        jnp.concatenate([wide_lo, thin_lo]), "gy", [(i, i + 1) for i in range(count - 1)]
    )
    from_hi = lax.ppermute(
        jnp.concatenate([wide_hi, thin_hi]), "gy", [(i + 1, i) for i in range(count - 1)]
    )
    split_lo = pairs_lo * cells_x * 2
    blank = jnp.zeros((channels - pairs_lo, cells_x, 1, depth), jnp.float32)
    cols_lo = jnp.concatenate(
        [
            from_lo[:split_lo].reshape((pairs_lo, cells_x, 2, depth)),
            jnp.concatenate(
                [blank, from_lo[split_lo:].reshape((-1, cells_x, 1, depth))], axis=2
            ),
        ]
    )
    split_hi = pairs_hi * cells_x * 2
    blank = jnp.zeros((channels - pairs_hi, cells_x, 1, depth), jnp.float32)
    cols_hi = jnp.concatenate(
        [
            from_hi[:split_hi].reshape((pairs_hi, cells_x, 2, depth)),
            jnp.concatenate(
                [from_hi[split_hi:].reshape((-1, cells_x, 1, depth)), blank], axis=2
            ),
        ]
    )
    tail = jnp.zeros((channels, cells_x, span_y - cells_y - 4, depth), jnp.float32)
    return jnp.concatenate([cols_lo, grown, cols_hi, tail], axis=2)


def local(
    fwd_now,
    fwd_prev,
    adj_now,
    adj_prev,
    lame_first,
    shear_mod,
    buoyancy,
    master_cell,
    master_lag,
    master_trace,
    receiver_cell,
    receiver_lag,
    receiver_trace,
):
    cells_x, cells_y, depth = lame_first.shape
    groups = lax.axis_size("grp")
    receivers = adj_now.shape[0]
    fields = receivers + 1
    width_y = cells_y * lax.axis_size("gy")
    start_x = lax.axis_index("gx") * cells_x
    start_y = lax.axis_index("gy") * cells_y
    grid = (cells_x, cells_y, depth)

    now = jnp.concatenate([fwd_now[None], adj_now]).reshape((fields * 3,) + grid)
    prev = jnp.concatenate([fwd_prev[None], adj_prev]).reshape((fields * 3,) + grid)
    comps = fields * 3
    stacked = jnp.concatenate([now, lame_first[None], shear_mod[None], prev, buoyancy[None]])
    span_y = 16 * ((cells_y + 4 + 15) // 16)
    grown = exchange_y(exchange_x(stacked, comps + 2, comps), comps + 2, comps, span_y)
    now_grown = grown[:comps].reshape((fields, 3) + grown.shape[1:])
    lame_grown = grown[comps]
    shear_grown = grown[comps + 1]
    prev_grown = grown[comps + 2 : 2 * comps + 2].reshape((fields, 3) + grown.shape[1:])
    buoy_grown = grown[2 * comps + 2]

    cells = jnp.concatenate([master_cell, receiver_cell])
    amps = [
        jnp.concatenate(
            [
                pick(master_trace[None], master_lag + instant),
                pick(receiver_trace, receiver_lag + instant),
            ]
        )
        for instant in range(STEPS)
    ]
    masks_wide = locate(cells, start_x - 1, start_y - 2, width_y, depth, cells_x + 2, span_y)
    inner = (slice(None), slice(1, 1 + cells_x), slice(2, 2 + cells_y))

    force0, strain0 = dense_stencil(now_grown, lame_grown, shear_grown)
    now_wide = now_grown[:, :, 1:-1]
    next_wide = advance(
        now_wide,
        prev_grown[:, :, 1:-1],
        force0,
        amps[0],
        masks_wide,
        buoy_grown[1:-1],
    )
    strain0 = strain0[:, :, 2 : 2 + cells_x, 2 : 2 + cells_y]

    force1, strain1 = dense_stencil(next_wide[1:], lame_grown[1:-1], shear_grown[1:-1])
    master1 = dense_stencil(next_wide[:1], lame_grown[1:-1], shear_grown[1:-1])[1]
    strain1 = strain1[:, :, 1 : 1 + cells_x, 2 : 2 + cells_y]
    master1 = master1[:, :, 1 : 1 + cells_x, 2 : 2 + cells_y]
    final = advance(
        next_wide[1:, :, 1 : 1 + cells_x],
        now_wide[1:, :, 1 : 1 + cells_x],
        force1,
        amps[1][1:],
        masks_wide[1:, 1 : 1 + cells_x],
        buoy_grown[2 : 2 + cells_x],
    )[:, :, :, 2 : 2 + cells_y]

    weights = jnp.array([1.0, 1.0, 1.0, 2.0, 2.0, 2.0], jnp.float32)[:, None, None, None]
    totals = jnp.zeros((2,) + grid, jnp.float32)
    for master, strain in ((strain0[0], strain0[1:]), (master1[0], strain1)):
        summed = jnp.sum(strain, axis=0)
        dilation_term = (master[0] + master[1] + master[2]) * (summed[0] + summed[1] + summed[2])
        shear_term = 2.0 * jnp.sum(weights * master * summed, axis=0)
        totals = totals + jnp.stack([dilation_term, shear_term])
    totals = totals * (1.0 / (STEPS * receivers * groups))

    share = depth // groups
    gathered = lax.all_to_all(totals, "grp", 3, 0, tiled=True)
    kernels = jnp.sum(gathered.reshape((groups, 2, cells_x, cells_y, share)), axis=0)
    return (final, kernels)


def solution(mesh):
    in_specs = (
        P(None, "gx", "gy", None),
        P(None, "gx", "gy", None),
        P("grp", None, "gx", "gy", None),
        P("grp", None, "gx", "gy", None),
        P("gx", "gy", None),
        P("gx", "gy", None),
        P("gx", "gy", None),
        P(),
        P(),
        P(),
        P("grp"),
        P("grp"),
        P("grp", None, None),
    )
    out_specs = (P("grp", None, "gx", "gy", None), P(None, "gx", "gy", "grp"))
    return jax.shard_map(local, mesh=mesh, in_specs=in_specs, out_specs=out_specs, check_vma=False)
```

```python
import jax
import jax.numpy as jnp
from jax import lax
from jax.sharding import PartitionSpec as P

STEPS = 2


time_step_sq = 0.0625


def with_halo(cells, sides, width):
    for axis, dim in sides:
        count = lax.axis_size(axis)
        ends = count - 1
        head = lax.slice_in_dim(cells, 0, width, axis=dim)
        tail = lax.slice_in_dim(cells, cells.shape[dim] - width, cells.shape[dim], axis=dim)
        cells = jnp.concatenate(
            [
                lax.ppermute(tail, axis, [(i, i + 1) for i in range(ends)]),
                cells,
                lax.ppermute(head, axis, [(i + 1, i) for i in range(ends)]),
            ],
            axis=dim,
        )
    return cells


def backward_diff(stress, axis):
    upper = stress[:, 1:, 1:, 1:]
    if axis == 1:
        lower = stress[:, :-1, 1:, 1:]
    elif axis == 2:
        lower = stress[:, 1:, :-1, 1:]
    else:
        lower = stress[:, 1:, 1:, :-1]
    return upper - lower


def strains_of(padded):
    span_x = padded.shape[2] - 2
    span_y = padded.shape[3] - 2
    span_z = padded.shape[4] - 2
    anchor = padded[:, :, : span_x + 1, : span_y + 1, : span_z + 1]
    grad_x = padded[:, :, 1:, : span_y + 1, : span_z + 1] - anchor
    grad_y = padded[:, :, : span_x + 1, 1:, : span_z + 1] - anchor
    grad_z = padded[:, :, : span_x + 1, : span_y + 1, 1:] - anchor
    strain_xx = grad_x[:, 0]
    strain_yy = grad_y[:, 1]
    strain_zz = grad_z[:, 2]
    strain_xy = 0.5 * (grad_y[:, 0] + grad_x[:, 1])
    strain_xz = 0.5 * (grad_z[:, 0] + grad_x[:, 2])
    strain_yz = 0.5 * (grad_z[:, 1] + grad_y[:, 2])
    return strain_xx, strain_yy, strain_zz, strain_xy, strain_xz, strain_yz


def stencil(padded, lame_pad, shear_pad):
    span_x = padded.shape[2] - 2
    span_y = padded.shape[3] - 2
    span_z = padded.shape[4] - 2
    strain_xx, strain_yy, strain_zz, strain_xy, strain_xz, strain_yz = strains_of(padded)
    lame = lame_pad[: span_x + 1, : span_y + 1, : span_z + 1]
    shear = shear_pad[: span_x + 1, : span_y + 1, : span_z + 1]
    dilation = strain_xx + strain_yy + strain_zz
    stress_xx = lame * dilation + 2.0 * shear * strain_xx
    stress_yy = lame * dilation + 2.0 * shear * strain_yy
    stress_zz = lame * dilation + 2.0 * shear * strain_zz
    stress_xy = 2.0 * shear * strain_xy
    stress_xz = 2.0 * shear * strain_xz
    stress_yz = 2.0 * shear * strain_yz
    force_x = (
        backward_diff(stress_xx, 1) + backward_diff(stress_xy, 2) + backward_diff(stress_xz, 3)
    )
    force_y = (
        backward_diff(stress_xy, 1) + backward_diff(stress_yy, 2) + backward_diff(stress_yz, 3)
    )
    force_z = (
        backward_diff(stress_xz, 1) + backward_diff(stress_yz, 2) + backward_diff(stress_zz, 3)
    )
    force = jnp.stack([force_x, force_y, force_z], axis=1)
    strain = jnp.stack([strain_xx, strain_yy, strain_zz, strain_xy, strain_xz, strain_yz], axis=1)
    return (force, strain[:, :, 1:, 1:, 1:])


def zpad(cells):
    widths = [(0, 0)] * (cells.ndim - 1) + [(1, 1)]
    return jnp.pad(cells, widths)


def locate(cells, start_x, start_y, width_y, depth, span_x, span_y):
    coord_x = cells // (width_y * depth) - start_x
    coord_y = cells // depth % width_y - start_y
    coord_z = cells % depth
    index_x = lax.broadcasted_iota(jnp.int32, (1, span_x, 1, 1), 1)
    index_y = lax.broadcasted_iota(jnp.int32, (1, 1, span_y, 1), 2)
    index_z = lax.broadcasted_iota(jnp.int32, (1, 1, 1, depth), 3)
    found = (
        (index_x == coord_x[:, None, None, None])
        & (index_y == coord_y[:, None, None, None])
        & (index_z == coord_z[:, None, None, None])
    )
    return found.astype(jnp.float32)


def pick(trace, lags):
    positions = lax.broadcasted_iota(jnp.int32, (1, trace.shape[1]), 1)
    chosen = positions == lags[:, None]
    return jnp.sum(jnp.where(chosen[:, :, None], trace, 0.0), axis=1)


def advance(current, earlier, force, amplitudes, masks, buoyancy):
    source = amplitudes[:, :, None, None, None] * masks[:, None]
    return 2.0 * current - earlier + time_step_sq * buoyancy * (force + source)


def exchange_x(stacked, pairs_lo, pairs_hi):
    channels, cells_x, cells_y, depth = stacked.shape
    plane = (cells_y, depth)
    count = lax.axis_size("gx")
    wide_lo = stacked[:pairs_lo, cells_x - 2 :].reshape((-1,) + plane)
    thin_lo = stacked[pairs_lo:, cells_x - 1 :].reshape((-1,) + plane)
    wide_hi = stacked[:pairs_hi, :2].reshape((-1,) + plane)
    thin_hi = stacked[pairs_hi:, :1].reshape((-1,) + plane)
    from_lo = lax.ppermute(
        jnp.concatenate([wide_lo, thin_lo]), "gx", [(i, i + 1) for i in range(count - 1)]
    )
    from_hi = lax.ppermute(
        jnp.concatenate([wide_hi, thin_hi]), "gx", [(i + 1, i) for i in range(count - 1)]
    )
    blank = jnp.zeros((channels - pairs_lo, 1) + plane, jnp.float32)
    rows_lo = jnp.concatenate(
        [
            from_lo[: pairs_lo * 2].reshape((pairs_lo, 2) + plane),
            jnp.concatenate([blank, from_lo[pairs_lo * 2 :].reshape((-1, 1) + plane)], axis=1),
        ]
    )
    blank = jnp.zeros((channels - pairs_hi, 1) + plane, jnp.float32)
    rows_hi = jnp.concatenate(
        [
            from_hi[: pairs_hi * 2].reshape((pairs_hi, 2) + plane),
            jnp.concatenate([from_hi[pairs_hi * 2 :].reshape((-1, 1) + plane), blank], axis=1),
        ]
    )
    return jnp.concatenate([rows_lo, stacked, rows_hi], axis=1)


def ahead(cells, axis):
    widths = [(0, 0)] * cells.ndim
    widths[axis] = (0, 1)
    return jnp.pad(lax.slice_in_dim(cells, 1, cells.shape[axis], axis=axis), widths)


def behind(cells, axis):
    widths = [(0, 0)] * cells.ndim
    widths[axis] = (1, 0)
    return jnp.pad(lax.slice_in_dim(cells, 0, cells.shape[axis] - 1, axis=axis), widths)


def up_z(cells):
    return ahead(cells, cells.ndim - 1)


def down_z(cells):
    return behind(cells, cells.ndim - 1)


def dense_stencil(cells, lame, shear):
    lower = cells[:, :, :-1]
    grad_x = cells[:, :, 1:] - lower
    grad_y = ahead(lower, 3) - lower
    grad_z = up_z(lower) - lower
    strain_xx = grad_x[:, 0]
    strain_yy = grad_y[:, 1]
    strain_zz = grad_z[:, 2]
    strain_xy = 0.5 * (grad_y[:, 0] + grad_x[:, 1])
    strain_xz = 0.5 * (grad_z[:, 0] + grad_x[:, 2])
    strain_yz = 0.5 * (grad_z[:, 1] + grad_y[:, 2])
    lame = lame[:-1]
    shear = shear[:-1]
    dilation = strain_xx + strain_yy + strain_zz
    stress_xx = lame * dilation + 2.0 * shear * strain_xx
    stress_yy = lame * dilation + 2.0 * shear * strain_yy
    stress_zz = lame * dilation + 2.0 * shear * strain_zz
    stress_xy = 2.0 * shear * strain_xy
    stress_xz = 2.0 * shear * strain_xz
    stress_yz = 2.0 * shear * strain_yz

    def diff_x(stress):
        return stress[:, 1:] - stress[:, :-1]

    def diff_y(stress):
        return (stress - behind(stress, 2))[:, 1:]

    def diff_z(stress):
        return (stress - down_z(stress))[:, 1:]

    force_x = diff_x(stress_xx) + diff_y(stress_xy) + diff_z(stress_xz)
    force_y = diff_x(stress_xy) + diff_y(stress_yy) + diff_z(stress_yz)
    force_z = diff_x(stress_xz) + diff_y(stress_yz) + diff_z(stress_zz)
    force = jnp.stack([force_x, force_y, force_z], axis=1)
    strain = jnp.stack([strain_xx, strain_yy, strain_zz, strain_xy, strain_xz, strain_yz], axis=1)
    return (force, strain)


def local(
    fwd_now,
    fwd_prev,
    adj_now,
    adj_prev,
    lame_first,
    shear_mod,
    buoyancy,
    master_cell,
    master_lag,
    master_trace,
    receiver_cell,
    receiver_lag,
    receiver_trace,
):
    cells_x, cells_y, depth = lame_first.shape
    groups = lax.axis_size("grp")
    receivers = adj_now.shape[0]
    fields = receivers + 1
    width_y = cells_y * lax.axis_size("gy")
    start_x = lax.axis_index("gx") * cells_x
    start_y = lax.axis_index("gy") * cells_y
    grid = (cells_x, cells_y, depth)

    now = jnp.concatenate([fwd_now[None], adj_now]).reshape((fields * 3,) + grid)
    prev = jnp.concatenate([fwd_prev[None], adj_prev]).reshape((fields * 3,) + grid)
    comps = fields * 3
    stacked = jnp.concatenate([now, lame_first[None], shear_mod[None], prev, buoyancy[None]])
    grown = with_halo(exchange_x(stacked, comps + 2, comps), (("gy", 2),), 2)
    span_y = 16 * ((cells_y + 4 + 15) // 16)
    grown = jnp.pad(grown, ((0, 0), (0, 0), (0, span_y - cells_y - 4), (0, 0)))
    now_grown = grown[:comps].reshape((fields, 3) + grown.shape[1:])
    lame_grown = grown[comps]
    shear_grown = grown[comps + 1]
    prev_grown = grown[comps + 2 : 2 * comps + 2].reshape((fields, 3) + grown.shape[1:])
    buoy_grown = grown[2 * comps + 2]

    cells = jnp.concatenate([master_cell, receiver_cell])
    amps = [
        jnp.concatenate(
            [
                pick(master_trace[None], master_lag + instant),
                pick(receiver_trace, receiver_lag + instant),
            ]
        )
        for instant in range(STEPS)
    ]
    masks_wide = locate(cells, start_x - 1, start_y - 2, width_y, depth, cells_x + 2, span_y)
    inner = (slice(None), slice(1, 1 + cells_x), slice(2, 2 + cells_y))

    force0, strain0 = dense_stencil(now_grown, lame_grown, shear_grown)
    now_wide = now_grown[:, :, 1:-1]
    next_wide = advance(
        now_wide,
        prev_grown[:, :, 1:-1],
        force0,
        amps[0],
        masks_wide,
        buoy_grown[1:-1],
    )
    strain0 = strain0[:, :, 2 : 2 + cells_x, 2 : 2 + cells_y]

    force1, strain1 = dense_stencil(next_wide[1:], lame_grown[1:-1], shear_grown[1:-1])
    master1 = dense_stencil(next_wide[:1], lame_grown[1:-1], shear_grown[1:-1])[1]
    strain1 = strain1[:, :, 1 : 1 + cells_x, 2 : 2 + cells_y]
    master1 = master1[:, :, 1 : 1 + cells_x, 2 : 2 + cells_y]
    final = advance(
        next_wide[1:, :, 1 : 1 + cells_x],
        now_wide[1:, :, 1 : 1 + cells_x],
        force1,
        amps[1][1:],
        masks_wide[1:, 1 : 1 + cells_x],
        buoy_grown[2 : 2 + cells_x],
    )[:, :, :, 2 : 2 + cells_y]

    weights = jnp.array([1.0, 1.0, 1.0, 2.0, 2.0, 2.0], jnp.float32)[:, None, None, None]
    totals = jnp.zeros((2,) + grid, jnp.float32)
    for master, strain in ((strain0[0], strain0[1:]), (master1[0], strain1)):
        summed = jnp.sum(strain, axis=0)
        dilation_term = (master[0] + master[1] + master[2]) * (summed[0] + summed[1] + summed[2])
        shear_term = 2.0 * jnp.sum(weights * master * summed, axis=0)
        totals = totals + jnp.stack([dilation_term, shear_term])
    totals = totals * (1.0 / (STEPS * receivers * groups))

    share = depth // groups
    gathered = lax.all_to_all(totals, "grp", 3, 0, tiled=True)
    kernels = jnp.sum(gathered.reshape((groups, 2, cells_x, cells_y, share)), axis=0)
    return (final, kernels)


def solution(mesh):
    in_specs = (
        P(None, "gx", "gy", None),
        P(None, "gx", "gy", None),
        P("grp", None, "gx", "gy", None),
        P("grp", None, "gx", "gy", None),
        P("gx", "gy", None),
        P("gx", "gy", None),
        P("gx", "gy", None),
        P(),
        P(),
        P(),
        P("grp"),
        P("grp"),
        P("grp", None, None),
    )
    out_specs = (P("grp", None, "gx", "gy", None), P(None, "gx", "gy", "grp"))
    return jax.shard_map(local, mesh=mesh, in_specs=in_specs, out_specs=out_specs, check_vma=False)
```

```python
import jax
import jax.numpy as jnp
from jax import lax
from jax.sharding import PartitionSpec as P

STEPS = 2


time_step_sq = 0.0625


def with_halo(cells, sides, width):
    for axis, dim in sides:
        count = lax.axis_size(axis)
        ends = count - 1
        head = lax.slice_in_dim(cells, 0, width, axis=dim)
        tail = lax.slice_in_dim(cells, cells.shape[dim] - width, cells.shape[dim], axis=dim)
        cells = jnp.concatenate(
            [
                lax.ppermute(tail, axis, [(i, i + 1) for i in range(ends)]),
                cells,
                lax.ppermute(head, axis, [(i + 1, i) for i in range(ends)]),
            ],
            axis=dim,
        )
    return cells


def backward_diff(stress, axis):
    upper = stress[:, 1:, 1:, 1:]
    if axis == 1:
        lower = stress[:, :-1, 1:, 1:]
    elif axis == 2:
        lower = stress[:, 1:, :-1, 1:]
    else:
        lower = stress[:, 1:, 1:, :-1]
    return upper - lower


def strains_of(padded):
    span_x = padded.shape[2] - 2
    span_y = padded.shape[3] - 2
    span_z = padded.shape[4] - 2
    anchor = padded[:, :, : span_x + 1, : span_y + 1, : span_z + 1]
    grad_x = padded[:, :, 1:, : span_y + 1, : span_z + 1] - anchor
    grad_y = padded[:, :, : span_x + 1, 1:, : span_z + 1] - anchor
    grad_z = padded[:, :, : span_x + 1, : span_y + 1, 1:] - anchor
    strain_xx = grad_x[:, 0]
    strain_yy = grad_y[:, 1]
    strain_zz = grad_z[:, 2]
    strain_xy = 0.5 * (grad_y[:, 0] + grad_x[:, 1])
    strain_xz = 0.5 * (grad_z[:, 0] + grad_x[:, 2])
    strain_yz = 0.5 * (grad_z[:, 1] + grad_y[:, 2])
    return strain_xx, strain_yy, strain_zz, strain_xy, strain_xz, strain_yz


def stencil(padded, lame_pad, shear_pad):
    span_x = padded.shape[2] - 2
    span_y = padded.shape[3] - 2
    span_z = padded.shape[4] - 2
    strain_xx, strain_yy, strain_zz, strain_xy, strain_xz, strain_yz = strains_of(padded)
    lame = lame_pad[: span_x + 1, : span_y + 1, : span_z + 1]
    shear = shear_pad[: span_x + 1, : span_y + 1, : span_z + 1]
    dilation = strain_xx + strain_yy + strain_zz
    stress_xx = lame * dilation + 2.0 * shear * strain_xx
    stress_yy = lame * dilation + 2.0 * shear * strain_yy
    stress_zz = lame * dilation + 2.0 * shear * strain_zz
    stress_xy = 2.0 * shear * strain_xy
    stress_xz = 2.0 * shear * strain_xz
    stress_yz = 2.0 * shear * strain_yz
    force_x = (
        backward_diff(stress_xx, 1) + backward_diff(stress_xy, 2) + backward_diff(stress_xz, 3)
    )
    force_y = (
        backward_diff(stress_xy, 1) + backward_diff(stress_yy, 2) + backward_diff(stress_yz, 3)
    )
    force_z = (
        backward_diff(stress_xz, 1) + backward_diff(stress_yz, 2) + backward_diff(stress_zz, 3)
    )
    force = jnp.stack([force_x, force_y, force_z], axis=1)
    strain = jnp.stack([strain_xx, strain_yy, strain_zz, strain_xy, strain_xz, strain_yz], axis=1)
    return (force, strain[:, :, 1:, 1:, 1:])


def zpad(cells):
    widths = [(0, 0)] * (cells.ndim - 1) + [(1, 1)]
    return jnp.pad(cells, widths)


def locate(cells, start_x, start_y, width_y, depth, span_x, span_y):
    coord_x = cells // (width_y * depth) - start_x
    coord_y = cells // depth % width_y - start_y
    coord_z = cells % depth
    index_x = lax.broadcasted_iota(jnp.int32, (1, span_x, 1, 1), 1)
    index_y = lax.broadcasted_iota(jnp.int32, (1, 1, span_y, 1), 2)
    index_z = lax.broadcasted_iota(jnp.int32, (1, 1, 1, depth), 3)
    found = (
        (index_x == coord_x[:, None, None, None])
        & (index_y == coord_y[:, None, None, None])
        & (index_z == coord_z[:, None, None, None])
    )
    return found.astype(jnp.float32)


def pick(trace, lags):
    positions = lax.broadcasted_iota(jnp.int32, (1, trace.shape[1]), 1)
    chosen = positions == lags[:, None]
    return jnp.sum(jnp.where(chosen[:, :, None], trace, 0.0), axis=1)


def advance(current, earlier, force, amplitudes, masks, buoyancy):
    source = amplitudes[:, :, None, None, None] * masks[:, None]
    return 2.0 * current - earlier + time_step_sq * buoyancy * (force + source)


def exchange_x(stacked, pairs_lo, pairs_hi):
    channels, cells_x, cells_y, depth = stacked.shape
    plane = (cells_y, depth)
    count = lax.axis_size("gx")
    wide_lo = stacked[:pairs_lo, cells_x - 2 :].reshape((-1,) + plane)
    thin_lo = stacked[pairs_lo:, cells_x - 1 :].reshape((-1,) + plane)
    wide_hi = stacked[:pairs_hi, :2].reshape((-1,) + plane)
    thin_hi = stacked[pairs_hi:, :1].reshape((-1,) + plane)
    from_lo = lax.ppermute(
        jnp.concatenate([wide_lo, thin_lo]), "gx", [(i, i + 1) for i in range(count - 1)]
    )
    from_hi = lax.ppermute(
        jnp.concatenate([wide_hi, thin_hi]), "gx", [(i + 1, i) for i in range(count - 1)]
    )
    blank = jnp.zeros((channels - pairs_lo, 1) + plane, jnp.float32)
    rows_lo = jnp.concatenate(
        [
            from_lo[: pairs_lo * 2].reshape((pairs_lo, 2) + plane),
            jnp.concatenate([blank, from_lo[pairs_lo * 2 :].reshape((-1, 1) + plane)], axis=1),
        ]
    )
    blank = jnp.zeros((channels - pairs_hi, 1) + plane, jnp.float32)
    rows_hi = jnp.concatenate(
        [
            from_hi[: pairs_hi * 2].reshape((pairs_hi, 2) + plane),
            jnp.concatenate([from_hi[pairs_hi * 2 :].reshape((-1, 1) + plane), blank], axis=1),
        ]
    )
    return jnp.concatenate([rows_lo, stacked, rows_hi], axis=1)


def ahead(cells, axis):
    widths = [(0, 0)] * cells.ndim
    widths[axis] = (0, 1)
    return jnp.pad(lax.slice_in_dim(cells, 1, cells.shape[axis], axis=axis), widths)


def behind(cells, axis):
    widths = [(0, 0)] * cells.ndim
    widths[axis] = (1, 0)
    return jnp.pad(lax.slice_in_dim(cells, 0, cells.shape[axis] - 1, axis=axis), widths)


def up_z(cells):
    return ahead(cells, cells.ndim - 1)


def down_z(cells):
    return behind(cells, cells.ndim - 1)


def dense_stencil(cells, lame, shear):
    lower = cells[:, :, :-1]
    grad_x = cells[:, :, 1:] - lower
    grad_y = ahead(lower, 3) - lower
    grad_z = up_z(lower) - lower
    strain_xx = grad_x[:, 0]
    strain_yy = grad_y[:, 1]
    strain_zz = grad_z[:, 2]
    strain_xy = 0.5 * (grad_y[:, 0] + grad_x[:, 1])
    strain_xz = 0.5 * (grad_z[:, 0] + grad_x[:, 2])
    strain_yz = 0.5 * (grad_z[:, 1] + grad_y[:, 2])
    lame = lame[:-1]
    shear = shear[:-1]
    dilation = strain_xx + strain_yy + strain_zz
    stress_xx = lame * dilation + 2.0 * shear * strain_xx
    stress_yy = lame * dilation + 2.0 * shear * strain_yy
    stress_zz = lame * dilation + 2.0 * shear * strain_zz
    stress_xy = 2.0 * shear * strain_xy
    stress_xz = 2.0 * shear * strain_xz
    stress_yz = 2.0 * shear * strain_yz

    def diff_x(stress):
        return stress[:, 1:] - stress[:, :-1]

    def diff_y(stress):
        return (stress - behind(stress, 2))[:, 1:]

    def diff_z(stress):
        return (stress - down_z(stress))[:, 1:]

    force_x = diff_x(stress_xx) + diff_y(stress_xy) + diff_z(stress_xz)
    force_y = diff_x(stress_xy) + diff_y(stress_yy) + diff_z(stress_yz)
    force_z = diff_x(stress_xz) + diff_y(stress_yz) + diff_z(stress_zz)
    force = jnp.stack([force_x, force_y, force_z], axis=1)
    strain = jnp.stack([strain_xx, strain_yy, strain_zz, strain_xy, strain_xz, strain_yz], axis=1)
    return (force, strain)


def local(
    fwd_now,
    fwd_prev,
    adj_now,
    adj_prev,
    lame_first,
    shear_mod,
    buoyancy,
    master_cell,
    master_lag,
    master_trace,
    receiver_cell,
    receiver_lag,
    receiver_trace,
):
    cells_x, cells_y, depth = lame_first.shape
    groups = lax.axis_size("grp")
    receivers = adj_now.shape[0]
    fields = receivers + 1
    width_y = cells_y * lax.axis_size("gy")
    start_x = lax.axis_index("gx") * cells_x
    start_y = lax.axis_index("gy") * cells_y
    grid = (cells_x, cells_y, depth)

    comps = fields * 3
    stacked = jnp.concatenate(
        [
            fwd_now,
            adj_now.reshape((receivers * 3,) + grid),
            lame_first[None],
            shear_mod[None],
            fwd_prev,
            adj_prev.reshape((receivers * 3,) + grid),
            buoyancy[None],
        ]
    )
    grown = with_halo(exchange_x(stacked, comps + 2, comps), (("gy", 2),), 2)
    span_y = 16 * ((cells_y + 4 + 15) // 16)
    grown = jnp.pad(grown, ((0, 0), (0, 0), (0, span_y - cells_y - 4), (0, 0)))
    now_grown = grown[:comps].reshape((fields, 3) + grown.shape[1:])
    lame_grown = grown[comps]
    shear_grown = grown[comps + 1]
    prev_grown = grown[comps + 2 : 2 * comps + 2].reshape((fields, 3) + grown.shape[1:])
    buoy_grown = grown[2 * comps + 2]

    cells = jnp.concatenate([master_cell, receiver_cell])
    amps = [
        jnp.concatenate(
            [
                pick(master_trace[None], master_lag + instant),
                pick(receiver_trace, receiver_lag + instant),
            ]
        )
        for instant in range(STEPS)
    ]
    masks_wide = locate(cells, start_x - 1, start_y - 2, width_y, depth, cells_x + 2, span_y)
    inner = (slice(None), slice(1, 1 + cells_x), slice(2, 2 + cells_y))

    force0, strain0 = dense_stencil(now_grown, lame_grown, shear_grown)
    now_wide = now_grown[:, :, 1:-1]
    next_wide = advance(
        now_wide,
        prev_grown[:, :, 1:-1],
        force0,
        amps[0],
        masks_wide,
        buoy_grown[1:-1],
    )
    strain0 = strain0[:, :, 2 : 2 + cells_x, 2 : 2 + cells_y]

    force1, strain1 = dense_stencil(next_wide[1:], lame_grown[1:-1], shear_grown[1:-1])
    master1 = dense_stencil(next_wide[:1], lame_grown[1:-1], shear_grown[1:-1])[1]
    strain1 = strain1[:, :, 1 : 1 + cells_x, 2 : 2 + cells_y]
    master1 = master1[:, :, 1 : 1 + cells_x, 2 : 2 + cells_y]
    final = advance(
        next_wide[1:, :, 1 : 1 + cells_x],
        now_wide[1:, :, 1 : 1 + cells_x],
        force1,
        amps[1][1:],
        masks_wide[1:, 1 : 1 + cells_x],
        buoy_grown[2 : 2 + cells_x],
    )[:, :, :, 2 : 2 + cells_y]

    weights = jnp.array([1.0, 1.0, 1.0, 2.0, 2.0, 2.0], jnp.float32)[:, None, None, None]
    totals = jnp.zeros((2,) + grid, jnp.float32)
    for master, strain in ((strain0[0], strain0[1:]), (master1[0], strain1)):
        summed = jnp.sum(strain, axis=0)
        dilation_term = (master[0] + master[1] + master[2]) * (summed[0] + summed[1] + summed[2])
        shear_term = 2.0 * jnp.sum(weights * master * summed, axis=0)
        totals = totals + jnp.stack([dilation_term, shear_term])
    totals = totals * (1.0 / (STEPS * receivers * groups))

    share = depth // groups
    gathered = lax.all_to_all(totals, "grp", 3, 0, tiled=True)
    kernels = jnp.sum(gathered.reshape((groups, 2, cells_x, cells_y, share)), axis=0)
    return (final, kernels)


def solution(mesh):
    in_specs = (
        P(None, "gx", "gy", None),
        P(None, "gx", "gy", None),
        P("grp", None, "gx", "gy", None),
        P("grp", None, "gx", "gy", None),
        P("gx", "gy", None),
        P("gx", "gy", None),
        P("gx", "gy", None),
        P(),
        P(),
        P(),
        P("grp"),
        P("grp"),
        P("grp", None, None),
    )
    out_specs = (P("grp", None, "gx", "gy", None), P(None, "gx", "gy", "grp"))
    return jax.shard_map(local, mesh=mesh, in_specs=in_specs, out_specs=out_specs, check_vma=False)
```

```python
import jax
import jax.numpy as jnp
from jax import lax
from jax.sharding import PartitionSpec as P

STEPS = 2


time_step_sq = 0.0625


def with_halo(cells, sides, width):
    for axis, dim in sides:
        count = lax.axis_size(axis)
        ends = count - 1
        head = lax.slice_in_dim(cells, 0, width, axis=dim)
        tail = lax.slice_in_dim(cells, cells.shape[dim] - width, cells.shape[dim], axis=dim)
        cells = jnp.concatenate(
            [
                lax.ppermute(tail, axis, [(i, i + 1) for i in range(ends)]),
                cells,
                lax.ppermute(head, axis, [(i + 1, i) for i in range(ends)]),
            ],
            axis=dim,
        )
    return cells


def backward_diff(stress, axis):
    upper = stress[:, 1:, 1:, 1:]
    if axis == 1:
        lower = stress[:, :-1, 1:, 1:]
    elif axis == 2:
        lower = stress[:, 1:, :-1, 1:]
    else:
        lower = stress[:, 1:, 1:, :-1]
    return upper - lower


def strains_of(padded):
    span_x = padded.shape[2] - 2
    span_y = padded.shape[3] - 2
    span_z = padded.shape[4] - 2
    anchor = padded[:, :, : span_x + 1, : span_y + 1, : span_z + 1]
    grad_x = padded[:, :, 1:, : span_y + 1, : span_z + 1] - anchor
    grad_y = padded[:, :, : span_x + 1, 1:, : span_z + 1] - anchor
    grad_z = padded[:, :, : span_x + 1, : span_y + 1, 1:] - anchor
    strain_xx = grad_x[:, 0]
    strain_yy = grad_y[:, 1]
    strain_zz = grad_z[:, 2]
    strain_xy = 0.5 * (grad_y[:, 0] + grad_x[:, 1])
    strain_xz = 0.5 * (grad_z[:, 0] + grad_x[:, 2])
    strain_yz = 0.5 * (grad_z[:, 1] + grad_y[:, 2])
    return strain_xx, strain_yy, strain_zz, strain_xy, strain_xz, strain_yz


def stencil(padded, lame_pad, shear_pad):
    span_x = padded.shape[2] - 2
    span_y = padded.shape[3] - 2
    span_z = padded.shape[4] - 2
    strain_xx, strain_yy, strain_zz, strain_xy, strain_xz, strain_yz = strains_of(padded)
    lame = lame_pad[: span_x + 1, : span_y + 1, : span_z + 1]
    shear = shear_pad[: span_x + 1, : span_y + 1, : span_z + 1]
    dilation = strain_xx + strain_yy + strain_zz
    stress_xx = lame * dilation + 2.0 * shear * strain_xx
    stress_yy = lame * dilation + 2.0 * shear * strain_yy
    stress_zz = lame * dilation + 2.0 * shear * strain_zz
    stress_xy = 2.0 * shear * strain_xy
    stress_xz = 2.0 * shear * strain_xz
    stress_yz = 2.0 * shear * strain_yz
    force_x = (
        backward_diff(stress_xx, 1) + backward_diff(stress_xy, 2) + backward_diff(stress_xz, 3)
    )
    force_y = (
        backward_diff(stress_xy, 1) + backward_diff(stress_yy, 2) + backward_diff(stress_yz, 3)
    )
    force_z = (
        backward_diff(stress_xz, 1) + backward_diff(stress_yz, 2) + backward_diff(stress_zz, 3)
    )
    force = jnp.stack([force_x, force_y, force_z], axis=1)
    strain = jnp.stack([strain_xx, strain_yy, strain_zz, strain_xy, strain_xz, strain_yz], axis=1)
    return (force, strain[:, :, 1:, 1:, 1:])


def zpad(cells):
    widths = [(0, 0)] * (cells.ndim - 1) + [(1, 1)]
    return jnp.pad(cells, widths)


def locate(cells, start_x, start_y, width_y, depth, span_x, span_y):
    coord_x = cells // (width_y * depth) - start_x
    coord_y = cells // depth % width_y - start_y
    coord_z = cells % depth
    index_x = lax.broadcasted_iota(jnp.int32, (1, span_x, 1, 1), 1)
    index_y = lax.broadcasted_iota(jnp.int32, (1, 1, span_y, 1), 2)
    index_z = lax.broadcasted_iota(jnp.int32, (1, 1, 1, depth), 3)
    found = (
        (index_x == coord_x[:, None, None, None])
        & (index_y == coord_y[:, None, None, None])
        & (index_z == coord_z[:, None, None, None])
    )
    return found.astype(jnp.float32)


def pick(trace, lags):
    positions = lax.broadcasted_iota(jnp.int32, (1, trace.shape[1]), 1)
    chosen = positions == lags[:, None]
    return jnp.sum(jnp.where(chosen[:, :, None], trace, 0.0), axis=1)


def advance(current, earlier, force, amplitudes, masks, buoyancy):
    source = amplitudes[:, :, None, None, None] * masks[:, None]
    return 2.0 * current - earlier + time_step_sq * buoyancy * (force + source)


def exchange_x(stacked, pairs_lo, pairs_hi):
    channels, cells_x, cells_y, depth = stacked.shape
    plane = (cells_y, depth)
    count = lax.axis_size("gx")
    wide_lo = stacked[:pairs_lo, cells_x - 2 :].reshape((-1,) + plane)
    thin_lo = stacked[pairs_lo:, cells_x - 1 :].reshape((-1,) + plane)
    wide_hi = stacked[:pairs_hi, :2].reshape((-1,) + plane)
    thin_hi = stacked[pairs_hi:, :1].reshape((-1,) + plane)
    from_lo = lax.ppermute(
        jnp.concatenate([wide_lo, thin_lo]), "gx", [(i, i + 1) for i in range(count - 1)]
    )
    from_hi = lax.ppermute(
        jnp.concatenate([wide_hi, thin_hi]), "gx", [(i + 1, i) for i in range(count - 1)]
    )
    blank = jnp.zeros((channels - pairs_lo, 1) + plane, jnp.float32)
    rows_lo = jnp.concatenate(
        [
            from_lo[: pairs_lo * 2].reshape((pairs_lo, 2) + plane),
            jnp.concatenate([blank, from_lo[pairs_lo * 2 :].reshape((-1, 1) + plane)], axis=1),
        ]
    )
    blank = jnp.zeros((channels - pairs_hi, 1) + plane, jnp.float32)
    rows_hi = jnp.concatenate(
        [
            from_hi[: pairs_hi * 2].reshape((pairs_hi, 2) + plane),
            jnp.concatenate([from_hi[pairs_hi * 2 :].reshape((-1, 1) + plane), blank], axis=1),
        ]
    )
    return jnp.concatenate([rows_lo, stacked, rows_hi], axis=1)


def ahead(cells, axis):
    widths = [(0, 0)] * cells.ndim
    widths[axis] = (0, 1)
    return jnp.pad(lax.slice_in_dim(cells, 1, cells.shape[axis], axis=axis), widths)


def behind(cells, axis):
    widths = [(0, 0)] * cells.ndim
    widths[axis] = (1, 0)
    return jnp.pad(lax.slice_in_dim(cells, 0, cells.shape[axis] - 1, axis=axis), widths)


def up_z(cells):
    return ahead(cells, cells.ndim - 1)


def down_z(cells):
    return behind(cells, cells.ndim - 1)


def dense_stencil(cells, lame, shear):
    lower = cells[:, :, :-1]
    grad_x = cells[:, :, 1:] - lower
    grad_y = ahead(lower, 3) - lower
    grad_z = up_z(lower) - lower
    strain_xx = grad_x[:, 0]
    strain_yy = grad_y[:, 1]
    strain_zz = grad_z[:, 2]
    strain_xy = 0.5 * (grad_y[:, 0] + grad_x[:, 1])
    strain_xz = 0.5 * (grad_z[:, 0] + grad_x[:, 2])
    strain_yz = 0.5 * (grad_z[:, 1] + grad_y[:, 2])
    lame = lame[:-1]
    shear = shear[:-1]
    dilation = strain_xx + strain_yy + strain_zz
    stress_xx = lame * dilation + 2.0 * shear * strain_xx
    stress_yy = lame * dilation + 2.0 * shear * strain_yy
    stress_zz = lame * dilation + 2.0 * shear * strain_zz
    stress_xy = 2.0 * shear * strain_xy
    stress_xz = 2.0 * shear * strain_xz
    stress_yz = 2.0 * shear * strain_yz

    def diff_x(stress):
        return stress[:, 1:] - stress[:, :-1]

    def diff_y(stress):
        return (stress - behind(stress, 2))[:, 1:]

    def diff_z(stress):
        return (stress - down_z(stress))[:, 1:]

    force_x = diff_x(stress_xx) + diff_y(stress_xy) + diff_z(stress_xz)
    force_y = diff_x(stress_xy) + diff_y(stress_yy) + diff_z(stress_yz)
    force_z = diff_x(stress_xz) + diff_y(stress_yz) + diff_z(stress_zz)
    force = jnp.stack([force_x, force_y, force_z], axis=1)
    strain = jnp.stack([strain_xx, strain_yy, strain_zz, strain_xy, strain_xz, strain_yz], axis=1)
    return (force, strain)


def local(
    fwd_now,
    fwd_prev,
    adj_now,
    adj_prev,
    lame_first,
    shear_mod,
    buoyancy,
    master_cell,
    master_lag,
    master_trace,
    receiver_cell,
    receiver_lag,
    receiver_trace,
):
    cells_x, cells_y, depth = lame_first.shape
    groups = lax.axis_size("grp")
    receivers = adj_now.shape[0]
    fields = receivers + 1
    width_y = cells_y * lax.axis_size("gy")
    start_x = lax.axis_index("gx") * cells_x
    start_y = lax.axis_index("gy") * cells_y
    grid = (cells_x, cells_y, depth)

    now = jnp.concatenate([fwd_now[None], adj_now]).reshape((fields * 3,) + grid)
    prev = jnp.concatenate([fwd_prev[None], adj_prev]).reshape((fields * 3,) + grid)
    comps = fields * 3
    stacked = jnp.concatenate([now, lame_first[None], shear_mod[None], prev, buoyancy[None]])
    grown = with_halo(exchange_x(stacked, comps + 2, comps), (("gy", 2),), 2)
    span_y = 16 * ((cells_y + 4 + 15) // 16)
    grown = jnp.pad(grown, ((0, 0), (0, 0), (0, span_y - cells_y - 4), (0, 0)))
    now_grown = grown[:comps].reshape((fields, 3) + grown.shape[1:])
    lame_grown = grown[comps]
    shear_grown = grown[comps + 1]
    prev_grown = grown[comps + 2 : 2 * comps + 2].reshape((fields, 3) + grown.shape[1:])
    buoy_grown = grown[2 * comps + 2]

    cells = jnp.concatenate([master_cell, receiver_cell])
    amps = [
        jnp.concatenate(
            [
                pick(master_trace[None], master_lag + instant),
                pick(receiver_trace, receiver_lag + instant),
            ]
        )
        for instant in range(STEPS)
    ]
    masks_wide = locate(cells, start_x - 1, start_y - 2, width_y, depth, cells_x + 2, span_y)
    inner = (slice(None), slice(1, 1 + cells_x), slice(2, 2 + cells_y))

    force0, strain0 = dense_stencil(now_grown, lame_grown, shear_grown)
    now_wide = now_grown[:, :, 1:-1]
    next_wide = advance(
        now_wide,
        prev_grown[:, :, 1:-1],
        force0,
        amps[0],
        masks_wide,
        buoy_grown[1:-1],
    )
    strain0 = strain0[:, :, 2 : 2 + cells_x, 2 : 2 + cells_y]

    force1, strain1 = dense_stencil(next_wide[1:], lame_grown[1:-1], shear_grown[1:-1])
    master1 = dense_stencil(next_wide[:1], lame_grown[1:-1], shear_grown[1:-1])[1]
    strain1 = strain1[:, :, 1 : 1 + cells_x, 2 : 2 + cells_y]
    master1 = master1[:, :, 1 : 1 + cells_x, 2 : 2 + cells_y]
    final = advance(
        next_wide[1:, :, 1 : 1 + cells_x],
        now_wide[1:, :, 1 : 1 + cells_x],
        force1,
        amps[1][1:],
        masks_wide[1:, 1 : 1 + cells_x],
        buoy_grown[2 : 2 + cells_x],
    )[:, :, :, 2 : 2 + cells_y]

    weights = jnp.array([1.0, 1.0, 1.0, 2.0, 2.0, 2.0], jnp.float32)[:, None, None, None]
    totals = jnp.zeros((2,) + grid, jnp.float32)
    for master, strain in ((strain0[0], strain0[1:]), (master1[0], strain1)):
        summed = jnp.sum(strain, axis=0)
        dilation_term = (master[0] + master[1] + master[2]) * (summed[0] + summed[1] + summed[2])
        shear_term = 2.0 * jnp.sum(weights * master * summed, axis=0)
        totals = totals + jnp.stack([dilation_term, shear_term])
    totals = totals * (1.0 / (STEPS * receivers * groups))

    share = depth // groups
    chunk = 2 * cells_x * cells_y * share
    parts = jnp.moveaxis(totals.reshape((2, cells_x, cells_y, groups, share)), 3, 0)
    parts = parts.reshape((groups, chunk // 128, 128))
    gathered = lax.all_to_all(parts, "grp", 0, 0, tiled=True)
    kernels = jnp.sum(gathered.reshape((groups, chunk // 128, 128)), axis=0)
    kernels = kernels.reshape((2, cells_x, cells_y, share))
    return (final, kernels)


def solution(mesh):
    in_specs = (
        P(None, "gx", "gy", None),
        P(None, "gx", "gy", None),
        P("grp", None, "gx", "gy", None),
        P("grp", None, "gx", "gy", None),
        P("gx", "gy", None),
        P("gx", "gy", None),
        P("gx", "gy", None),
        P(),
        P(),
        P(),
        P("grp"),
        P("grp"),
        P("grp", None, None),
    )
    out_specs = (P("grp", None, "gx", "gy", None), P(None, "gx", "gy", "grp"))
    return jax.shard_map(local, mesh=mesh, in_specs=in_specs, out_specs=out_specs, check_vma=False)
```

```python
import jax
import jax.numpy as jnp
from jax import lax
from jax.sharding import PartitionSpec as P

STEPS = 2


time_step_sq = 0.0625


def with_halo(cells, sides, width):
    for axis, dim in sides:
        count = lax.axis_size(axis)
        ends = count - 1
        head = lax.slice_in_dim(cells, 0, width, axis=dim)
        tail = lax.slice_in_dim(cells, cells.shape[dim] - width, cells.shape[dim], axis=dim)
        cells = jnp.concatenate(
            [
                lax.ppermute(tail, axis, [(i, i + 1) for i in range(ends)]),
                cells,
                lax.ppermute(head, axis, [(i + 1, i) for i in range(ends)]),
            ],
            axis=dim,
        )
    return cells


def backward_diff(stress, axis):
    upper = stress[:, 1:, 1:, 1:]
    if axis == 1:
        lower = stress[:, :-1, 1:, 1:]
    elif axis == 2:
        lower = stress[:, 1:, :-1, 1:]
    else:
        lower = stress[:, 1:, 1:, :-1]
    return upper - lower


def strains_of(padded):
    span_x = padded.shape[2] - 2
    span_y = padded.shape[3] - 2
    span_z = padded.shape[4] - 2
    anchor = padded[:, :, : span_x + 1, : span_y + 1, : span_z + 1]
    grad_x = padded[:, :, 1:, : span_y + 1, : span_z + 1] - anchor
    grad_y = padded[:, :, : span_x + 1, 1:, : span_z + 1] - anchor
    grad_z = padded[:, :, : span_x + 1, : span_y + 1, 1:] - anchor
    strain_xx = grad_x[:, 0]
    strain_yy = grad_y[:, 1]
    strain_zz = grad_z[:, 2]
    strain_xy = 0.5 * (grad_y[:, 0] + grad_x[:, 1])
    strain_xz = 0.5 * (grad_z[:, 0] + grad_x[:, 2])
    strain_yz = 0.5 * (grad_z[:, 1] + grad_y[:, 2])
    return strain_xx, strain_yy, strain_zz, strain_xy, strain_xz, strain_yz


def stencil(padded, lame_pad, shear_pad):
    span_x = padded.shape[2] - 2
    span_y = padded.shape[3] - 2
    span_z = padded.shape[4] - 2
    strain_xx, strain_yy, strain_zz, strain_xy, strain_xz, strain_yz = strains_of(padded)
    lame = lame_pad[: span_x + 1, : span_y + 1, : span_z + 1]
    shear = shear_pad[: span_x + 1, : span_y + 1, : span_z + 1]
    dilation = strain_xx + strain_yy + strain_zz
    stress_xx = lame * dilation + 2.0 * shear * strain_xx
    stress_yy = lame * dilation + 2.0 * shear * strain_yy
    stress_zz = lame * dilation + 2.0 * shear * strain_zz
    stress_xy = 2.0 * shear * strain_xy
    stress_xz = 2.0 * shear * strain_xz
    stress_yz = 2.0 * shear * strain_yz
    force_x = (
        backward_diff(stress_xx, 1) + backward_diff(stress_xy, 2) + backward_diff(stress_xz, 3)
    )
    force_y = (
        backward_diff(stress_xy, 1) + backward_diff(stress_yy, 2) + backward_diff(stress_yz, 3)
    )
    force_z = (
        backward_diff(stress_xz, 1) + backward_diff(stress_yz, 2) + backward_diff(stress_zz, 3)
    )
    force = jnp.stack([force_x, force_y, force_z], axis=1)
    strain = jnp.stack([strain_xx, strain_yy, strain_zz, strain_xy, strain_xz, strain_yz], axis=1)
    return (force, strain[:, :, 1:, 1:, 1:])


def zpad(cells):
    widths = [(0, 0)] * (cells.ndim - 1) + [(1, 1)]
    return jnp.pad(cells, widths)


def locate(cells, start_x, start_y, width_y, depth, span_x, span_y):
    coord_x = cells // (width_y * depth) - start_x
    coord_y = cells // depth % width_y - start_y
    coord_z = cells % depth
    index_x = lax.broadcasted_iota(jnp.int32, (1, span_x, 1, 1), 1)
    index_y = lax.broadcasted_iota(jnp.int32, (1, 1, span_y, 1), 2)
    index_z = lax.broadcasted_iota(jnp.int32, (1, 1, 1, depth), 3)
    found = (
        (index_x == coord_x[:, None, None, None])
        & (index_y == coord_y[:, None, None, None])
        & (index_z == coord_z[:, None, None, None])
    )
    return found.astype(jnp.float32)


def pick(trace, lags):
    positions = lax.broadcasted_iota(jnp.int32, (1, trace.shape[1]), 1)
    chosen = positions == lags[:, None]
    return jnp.sum(jnp.where(chosen[:, :, None], trace, 0.0), axis=1)


def advance(current, earlier, force, amplitudes, masks, buoyancy):
    source = amplitudes[:, :, None, None, None] * masks[:, None]
    return 2.0 * current - earlier + time_step_sq * buoyancy * (force + source)


def exchange_x(stacked, pairs_lo, pairs_hi):
    channels, cells_x, cells_y, depth = stacked.shape
    plane = (cells_y, depth)
    count = lax.axis_size("gx")
    wide_lo = stacked[:pairs_lo, cells_x - 2 :].reshape((-1,) + plane)
    thin_lo = stacked[pairs_lo:, cells_x - 1 :].reshape((-1,) + plane)
    wide_hi = stacked[:pairs_hi, :2].reshape((-1,) + plane)
    thin_hi = stacked[pairs_hi:, :1].reshape((-1,) + plane)
    from_lo = lax.ppermute(
        jnp.concatenate([wide_lo, thin_lo]), "gx", [(i, i + 1) for i in range(count - 1)]
    )
    from_hi = lax.ppermute(
        jnp.concatenate([wide_hi, thin_hi]), "gx", [(i + 1, i) for i in range(count - 1)]
    )
    blank = jnp.zeros((channels - pairs_lo, 1) + plane, jnp.float32)
    rows_lo = jnp.concatenate(
        [
            from_lo[: pairs_lo * 2].reshape((pairs_lo, 2) + plane),
            jnp.concatenate([blank, from_lo[pairs_lo * 2 :].reshape((-1, 1) + plane)], axis=1),
        ]
    )
    blank = jnp.zeros((channels - pairs_hi, 1) + plane, jnp.float32)
    rows_hi = jnp.concatenate(
        [
            from_hi[: pairs_hi * 2].reshape((pairs_hi, 2) + plane),
            jnp.concatenate([from_hi[pairs_hi * 2 :].reshape((-1, 1) + plane), blank], axis=1),
        ]
    )
    return jnp.concatenate([rows_lo, stacked, rows_hi], axis=1)


def ahead(cells, axis):
    widths = [(0, 0)] * cells.ndim
    widths[axis] = (0, 1)
    return jnp.pad(lax.slice_in_dim(cells, 1, cells.shape[axis], axis=axis), widths)


def behind(cells, axis):
    widths = [(0, 0)] * cells.ndim
    widths[axis] = (1, 0)
    return jnp.pad(lax.slice_in_dim(cells, 0, cells.shape[axis] - 1, axis=axis), widths)


def up_z(cells):
    return ahead(cells, cells.ndim - 1)


def down_z(cells):
    return behind(cells, cells.ndim - 1)


def dense_stencil(cells, lame, shear):
    lower = cells[:, :, :-1]
    grad_x = cells[:, :, 1:] - lower
    grad_y = ahead(lower, 3) - lower
    grad_z = up_z(lower) - lower
    strain_xx = grad_x[:, 0]
    strain_yy = grad_y[:, 1]
    strain_zz = grad_z[:, 2]
    strain_xy = 0.5 * (grad_y[:, 0] + grad_x[:, 1])
    strain_xz = 0.5 * (grad_z[:, 0] + grad_x[:, 2])
    strain_yz = 0.5 * (grad_z[:, 1] + grad_y[:, 2])
    lame = lame[:-1]
    shear = shear[:-1]
    dilation = strain_xx + strain_yy + strain_zz
    stress_xx = lame * dilation + 2.0 * shear * strain_xx
    stress_yy = lame * dilation + 2.0 * shear * strain_yy
    stress_zz = lame * dilation + 2.0 * shear * strain_zz
    stress_xy = 2.0 * shear * strain_xy
    stress_xz = 2.0 * shear * strain_xz
    stress_yz = 2.0 * shear * strain_yz

    def diff_x(stress):
        return stress[:, 1:] - stress[:, :-1]

    def diff_y(stress):
        return (stress - behind(stress, 2))[:, 1:]

    def diff_z(stress):
        return (stress - down_z(stress))[:, 1:]

    force_x = diff_x(stress_xx) + diff_y(stress_xy) + diff_z(stress_xz)
    force_y = diff_x(stress_xy) + diff_y(stress_yy) + diff_z(stress_yz)
    force_z = diff_x(stress_xz) + diff_y(stress_yz) + diff_z(stress_zz)
    force = jnp.stack([force_x, force_y, force_z], axis=1)
    strain = jnp.stack([strain_xx, strain_yy, strain_zz, strain_xy, strain_xz, strain_yz], axis=1)
    return (force, strain)


def local(
    fwd_now,
    fwd_prev,
    adj_now,
    adj_prev,
    lame_first,
    shear_mod,
    buoyancy,
    master_cell,
    master_lag,
    master_trace,
    receiver_cell,
    receiver_lag,
    receiver_trace,
):
    cells_x, cells_y, depth = lame_first.shape
    groups = lax.axis_size("grp")
    receivers = adj_now.shape[0]
    fields = receivers + 1
    width_y = cells_y * lax.axis_size("gy")
    start_x = lax.axis_index("gx") * cells_x
    start_y = lax.axis_index("gy") * cells_y
    grid = (cells_x, cells_y, depth)

    now = jnp.concatenate([fwd_now[None], adj_now]).reshape((fields * 3,) + grid)
    prev = jnp.concatenate([fwd_prev[None], adj_prev]).reshape((fields * 3,) + grid)
    comps = fields * 3
    stacked = jnp.concatenate([now, lame_first[None], shear_mod[None], prev, buoyancy[None]])
    grown = with_halo(exchange_x(stacked, comps + 2, comps), (("gy", 2),), 2)
    span_y = 16 * ((cells_y + 4 + 15) // 16)
    grown = jnp.pad(grown, ((0, 0), (0, 0), (0, span_y - cells_y - 4), (0, 0)))
    now_grown = grown[:comps].reshape((fields, 3) + grown.shape[1:])
    lame_grown = grown[comps]
    shear_grown = grown[comps + 1]
    prev_grown = grown[comps + 2 : 2 * comps + 2].reshape((fields, 3) + grown.shape[1:])
    buoy_grown = grown[2 * comps + 2]

    cells = jnp.concatenate([master_cell, receiver_cell])
    amps = [
        jnp.concatenate(
            [
                pick(master_trace[None], master_lag + instant),
                pick(receiver_trace, receiver_lag + instant),
            ]
        )
        for instant in range(STEPS)
    ]
    masks_wide = locate(cells, start_x - 1, start_y - 2, width_y, depth, cells_x + 2, span_y)
    inner = (slice(None), slice(1, 1 + cells_x), slice(2, 2 + cells_y))

    force0, strain0 = dense_stencil(now_grown, lame_grown, shear_grown)
    now_wide = now_grown[:, :, 1:-1]
    next_wide = advance(
        now_wide,
        prev_grown[:, :, 1:-1],
        force0,
        amps[0],
        masks_wide,
        buoy_grown[1:-1],
    )
    strain0 = strain0[:, :, 2 : 2 + cells_x, 2 : 2 + cells_y]

    force1, strain1 = dense_stencil(next_wide[1:], lame_grown[1:-1], shear_grown[1:-1])
    master1 = dense_stencil(next_wide[:1], lame_grown[1:-1], shear_grown[1:-1])[1]
    strain1 = strain1[:, :, 1 : 1 + cells_x, 2 : 2 + cells_y]
    master1 = master1[:, :, 1 : 1 + cells_x, 2 : 2 + cells_y]
    final = advance(
        next_wide[1:, :, 1 : 1 + cells_x],
        now_wide[1:, :, 1 : 1 + cells_x],
        force1,
        amps[1][1:],
        masks_wide[1:, 1 : 1 + cells_x],
        buoy_grown[2 : 2 + cells_x],
    )[:, :, :, 2 : 2 + cells_y]

    weights = jnp.array([1.0, 1.0, 1.0, 2.0, 2.0, 2.0], jnp.float32)[:, None, None, None]
    totals = jnp.zeros((2,) + grid, jnp.float32)
    for master, strain in ((strain0[0], strain0[1:]), (master1[0], strain1)):
        summed = jnp.sum(strain, axis=0)
        dilation_term = (master[0] + master[1] + master[2]) * (summed[0] + summed[1] + summed[2])
        shear_term = 2.0 * jnp.sum(weights * master * summed, axis=0)
        totals = totals + jnp.stack([dilation_term, shear_term])
    totals = totals * (1.0 / (STEPS * receivers * groups))

    share = depth // groups
    chunk = 2 * cells_x * cells_y * share
    totals = lax.optimization_barrier(totals)
    parts = jnp.moveaxis(totals.reshape((2, cells_x, cells_y, groups, share)), 3, 0)
    parts = parts.reshape((groups, chunk // 128, 128))
    gathered = lax.all_to_all(parts, "grp", 0, 0, tiled=True)
    kernels = jnp.sum(gathered.reshape((groups, chunk // 128, 128)), axis=0)
    kernels = kernels.reshape((2, cells_x, cells_y, share))
    return (final, kernels)


def solution(mesh):
    in_specs = (
        P(None, "gx", "gy", None),
        P(None, "gx", "gy", None),
        P("grp", None, "gx", "gy", None),
        P("grp", None, "gx", "gy", None),
        P("gx", "gy", None),
        P("gx", "gy", None),
        P("gx", "gy", None),
        P(),
        P(),
        P(),
        P("grp"),
        P("grp"),
        P("grp", None, None),
    )
    out_specs = (P("grp", None, "gx", "gy", None), P(None, "gx", "gy", "grp"))
    return jax.shard_map(local, mesh=mesh, in_specs=in_specs, out_specs=out_specs, check_vma=False)
```
